256 devices in a mesh: seq: 16 (over y, x), chan: 16 (over z, core).
Axes of the slice: x: 4, y: 4, z: 8, core: 2. Of those that a mesh axis runs over, the one named last changes fastest.
Arguments:
- layer_input: bfloat16 [2048, 8192], P('seq', 'chan'), may hold values from -6 to 6
- value_pre: bfloat16 [2048, 8192], P('seq', 'chan'), may hold values from -6 to 6
- gate_act: bfloat16 [2048, 8192], P('seq', 'chan'), may hold values from -6 to 6
- key_act: bfloat16 [2048, 8192], P('seq', 'chan'), may hold values from -6 to 6
- short_taps: float32 [3, 8192], P(None, 'chan'), may hold values from -3 to 3
- long_filter: float32 [2048, 8192], P('seq', 'chan'), may hold values from -0.125 to 0.125
- grad_out: bfloat16 [2048, 8192], P('seq', 'chan'), may hold values from -6 to 6
Outputs:
- grad_gate: bfloat16 [2048, 8192], P('seq', 'chan')
- grad_key: bfloat16 [2048, 8192], P('seq', 'chan')
- grad_value: bfloat16 [2048, 8192], P('seq', 'chan')
- grad_taps: float32 [3, 8192], P(None, 'chan')
- grad_filter: float32 [2048, 8192], P('seq', 'chan')
- grad_proj: float32 [8192, 8192], P('chan', 'seq')
The draws below stay inside these ranges and needn't reach their ends.
All inputs are finite; a program needn't handle non-finite values.
Results may differ from the reference program's by a relative error of at most 0.0029.
Values may be sent and summed in bfloat16 or wider, within the bound.
No kernel may reach another device: no remote copies, remote signals or barrier semaphores. Data moves between devices by JAX's collectives and lax.ppermute only.
A program may use at most 128 MiB of HBM per device.

```python
import jax
import jax.numpy as jnp
from jax import lax

D = 8192
TAPS = 3
TOK_DEV = 128
SEQ_LEN = 2048
N_SEQ = 16
N_CHAN = 16


def block_scale(stream_key, shape, pieces, least, largest):
    def one(position, parts):
        draws = jax.random.uniform(jax.random.fold_in(jax.random.fold_in(stream_key, 6), position), (parts,), jnp.float32, least / len(pieces), largest / len(pieces))
        return jnp.repeat(jnp.exp(draws), shape[position] // parts).reshape((-1,) + (1,) * (len(shape) - position - 1))

    level = one(*pieces[0])
    for cut in pieces[1:]:
        level = level * one(*cut)
    return level


def gaussian(rng, shape, width, limit, cuts=(), dtype=jnp.bfloat16):
    values = jax.random.normal(rng, shape, jnp.float32) * width
    if len(cuts) > 0:
        values = block_scale(rng, shape, cuts, -0.22, 0.18) * values
    return jnp.clip(values, min=-limit, max=limit).astype(dtype)


def setup_inputs(seed: int = 0) -> dict:
    keys = jax.random.split(jax.random.key(seed), 8)
    return {
        "layer_input": gaussian(keys[0], (SEQ_LEN, D), 1.0, 6.0, ((0, 16), (1, 16))),
        "value_pre": gaussian(keys[1], (SEQ_LEN, D), 1.0, 6.0, ((0, 16), (1, 16))),
        "gate_act": gaussian(keys[2], (SEQ_LEN, D), 1.0, 6.0, ((0, 16), (1, 16))),
        "key_act": gaussian(keys[3], (SEQ_LEN, D), 1.0, 6.0, ((0, 16), (1, 16))),
        "short_taps": gaussian(keys[4], (TAPS, D), 0.5, 3.0, ((1, 16),), jnp.float32),
        "long_filter": gaussian(keys[5], (SEQ_LEN, D), SEQ_LEN ** -0.5, 0.125, ((0, 16), (1, 16)), jnp.float32),
        "grad_out": gaussian(keys[6], (SEQ_LEN, D), 1.0, 6.0, ((0, 16), (1, 16))),
    }


def long_part(filt_blk, signal_blk, grad_blk):
    length_seq = filt_blk.shape[0]
    size_total = 2 * length_seq
    filt_hat = jnp.fft.fft(filt_blk, n=size_total, axis=0)
    signal_hat = jnp.fft.fft(signal_blk, n=size_total, axis=0)
    grad_hat = jnp.fft.fft(grad_blk, n=size_total, axis=0)
    mix_out = jnp.real(jnp.fft.ifft(filt_hat * signal_hat, axis=0))[:length_seq]
    grad_signal = jnp.real(jnp.fft.ifft(jnp.conj(filt_hat) * grad_hat, axis=0))[:length_seq]
    grad_filter = jnp.real(jnp.fft.ifft(jnp.conj(signal_hat) * grad_hat, axis=0))[:length_seq]
    return (mix_out.astype(jnp.float32), grad_signal.astype(jnp.float32), grad_filter.astype(jnp.float32))


def reference(layer_input, value_pre, gate_act, key_act, short_taps, long_filter, grad_out):
    extended = jnp.pad(value_pre.astype(jnp.float32), ((TAPS - 1, 0), (0, 0)))
    conv_val = jnp.zeros((SEQ_LEN, D), jnp.float32)
    for tap_index in range(TAPS):
        offset_row = TAPS - 1 - tap_index
        conv_val = conv_val + short_taps[tap_index] * extended[offset_row:offset_row + SEQ_LEN]
    signal = key_act.astype(jnp.float32) * conv_val
    grad_mix = grad_out.astype(jnp.float32) * gate_act.astype(jnp.float32)
    block_width = D // N_CHAN
    blocks = D // block_width

    def to_blocks(matrix_in):
        return matrix_in.reshape(SEQ_LEN, blocks, block_width).transpose(1, 0, 2)

    def from_blocks(matrix_in):
        return matrix_in.transpose(1, 0, 2).reshape(SEQ_LEN, D)

    def one_block(block_trio):
        return long_part(block_trio[0], block_trio[1], block_trio[2])

    mix_blocks, back_blocks, filt_blocks = lax.map(one_block, (to_blocks(long_filter), to_blocks(signal), to_blocks(grad_mix)))
    mix_out = from_blocks(mix_blocks)
    grad_signal = from_blocks(back_blocks)
    grad_filter = from_blocks(filt_blocks)
    grad_gate = (grad_out.astype(jnp.float32) * mix_out).astype(jnp.bfloat16)
    grad_key = (grad_signal * conv_val).astype(jnp.bfloat16)
    grad_conv = grad_signal * key_act.astype(jnp.float32)
    padded_tail = jnp.pad(grad_conv, ((0, TAPS - 1), (0, 0)))
    value_sum = jnp.zeros((SEQ_LEN, D), jnp.float32)
    for tap_index in range(TAPS):
        value_sum = value_sum + short_taps[tap_index] * padded_tail[tap_index:tap_index + SEQ_LEN]
    grad_value = value_sum.astype(jnp.bfloat16)
    tap_rows = []
    for tap_index in range(TAPS):
        offset_row = TAPS - 1 - tap_index
        tap_rows.append(jnp.sum(grad_conv * extended[offset_row:offset_row + SEQ_LEN], axis=0))
    grad_taps = jnp.stack(tap_rows, axis=0)
    input_blocks = layer_input.astype(jnp.float32).reshape(N_SEQ, TOK_DEV, D)
    value_blocks = grad_value.astype(jnp.float32).reshape(N_SEQ, TOK_DEV, D)

    def add_block(running, block_pair):
        block_sum = jnp.dot(block_pair[0].T, block_pair[1], preferred_element_type=jnp.float32, precision=lax.Precision.HIGHEST)
        return running + block_sum, None

    grad_proj, _ = lax.scan(add_block, jnp.zeros((D, D), jnp.float32), (input_blocks, value_blocks))
    return (grad_gate, grad_key, grad_value, grad_taps, grad_filter, grad_proj)
```

```python
import jax
import jax.numpy as jnp
from jax import lax
from jax.sharding import PartitionSpec as P

F32 = jnp.float32
BF16 = jnp.bfloat16


def long_part(filt_blk, signal_blk, grad_blk):
    length_seq = filt_blk.shape[0]
    size_total = 2 * length_seq
    filt_hat = jnp.fft.rfft(filt_blk, n=size_total, axis=0)
    signal_hat = jnp.fft.rfft(signal_blk, n=size_total, axis=0)
    grad_hat = jnp.fft.rfft(grad_blk, n=size_total, axis=0)
    mix_out = jnp.fft.irfft(filt_hat * signal_hat, n=size_total, axis=0)[:length_seq]
    grad_signal = jnp.fft.irfft(jnp.conj(filt_hat) * grad_hat, n=size_total, axis=0)[:length_seq]
    grad_filter = jnp.fft.irfft(jnp.conj(signal_hat) * grad_hat, n=size_total, axis=0)[:length_seq]
    return (mix_out.astype(F32), grad_signal.astype(F32), grad_filter.astype(F32))


def on_device(layer_input, value_pre, gate_act, key_act, short_taps, long_filter, grad_out):
    n_seq = lax.axis_size("seq")
    n_chan = lax.axis_size("chan")
    me = lax.axis_index("seq")
    tap_count = short_taps.shape[0]
    sub = value_pre.shape[1] // n_seq

    inputs_all = lax.all_gather(layer_input, "seq", axis=0, tiled=True)

    halves = jnp.stack([value_pre, gate_act, key_act, grad_out])
    halves = lax.all_to_all(halves, "seq", split_axis=2, concat_axis=1, tiled=True)
    filt = lax.all_to_all(long_filter, "seq", split_axis=1, concat_axis=0, tiled=True)
    value_t = halves[0].astype(F32)
    gate_t = halves[1].astype(F32)
    key_t = halves[2].astype(F32)
    gout_t = halves[3].astype(F32)
    taps = lax.dynamic_slice_in_dim(short_taps, me * sub, sub, axis=1)
    length = value_t.shape[0]

    extended = jnp.pad(value_t, ((tap_count - 1, 0), (0, 0)))
    conv_val = jnp.zeros(value_t.shape, F32)
    for tap_index in range(tap_count):
        offset_row = tap_count - 1 - tap_index
        conv_val = conv_val + taps[tap_index] * extended[offset_row:offset_row + length]
    signal = key_t * conv_val
    grad_mix = gout_t * gate_t
    mix_out, grad_signal, grad_filter = long_part(filt, signal, grad_mix)
    grad_gate = (gout_t * mix_out).astype(BF16)
    grad_key = (grad_signal * conv_val).astype(BF16)
    grad_conv = grad_signal * key_t
    padded_tail = jnp.pad(grad_conv, ((0, tap_count - 1), (0, 0)))
    value_sum = jnp.zeros(grad_conv.shape, F32)
    for tap_index in range(tap_count):
        value_sum = value_sum + taps[tap_index] * padded_tail[tap_index:tap_index + length]
    grad_value = value_sum.astype(BF16)
    tap_rows = []
    for tap_index in range(tap_count):
        offset_row = tap_count - 1 - tap_index
        tap_rows.append(jnp.sum(grad_conv * extended[offset_row:offset_row + length], axis=0))
    grad_taps = lax.all_gather(jnp.stack(tap_rows, axis=0), "seq", axis=1, tiled=True)

    outs = jnp.stack([grad_gate, grad_key, grad_value])
    outs = lax.all_to_all(outs, "seq", split_axis=1, concat_axis=2, tiled=True)
    grad_filter = lax.all_to_all(grad_filter, "seq", split_axis=0, concat_axis=1, tiled=True)

    swap = [(a * n_chan + b, b * n_chan + a) for a in range(n_seq) for b in range(n_chan)]
    value_swapped = lax.ppermute(grad_value, ("seq", "chan"), swap)
    value_cols = lax.all_gather(value_swapped, "chan", axis=1, tiled=True)
    grad_proj = lax.dot_general(
        inputs_all, value_cols, (((0,), (0,)), ((), ())), preferred_element_type=F32
    )
    return (outs[0], outs[1], outs[2], grad_taps, grad_filter, grad_proj)


def solution(mesh):
    assert mesh.shape["seq"] == mesh.shape["chan"]
    in_specs = (
        P("seq", "chan"),
        P("seq", "chan"),
        P("seq", "chan"),
        P("seq", "chan"),
        P(None, "chan"),
        P("seq", "chan"),
        P("seq", "chan"),
    )
    out_specs = (
        P("seq", "chan"),
        P("seq", "chan"),
        P("seq", "chan"),
        P(None, "chan"),
        P("seq", "chan"),
        P("chan", "seq"),
    )
    return jax.shard_map(
        on_device, mesh=mesh, in_specs=in_specs, out_specs=out_specs, check_vma=False
    )
```

```python
import numpy as np

import jax
import jax.numpy as jnp
from jax import lax
from jax.sharding import PartitionSpec as P

F32 = jnp.float32
BF16 = jnp.bfloat16
PRECISE = lax.Precision.HIGHEST


def angles(rows, cols, period):
    product = np.outer(np.arange(rows), np.arange(cols)) % period
    return product.astype(np.float64) * (2.0 * np.pi / period)


def dft_tables(blocks, width):
    freq_blocks = 2 * blocks
    total = freq_blocks * width
    outer = angles(freq_blocks, blocks, freq_blocks)
    stage_a = np.concatenate([np.cos(outer), -np.sin(outer)], axis=0)
    twist = angles(freq_blocks, width, total)
    twist_cos = np.cos(twist)[:, None, None, :]
    twist_sin = np.sin(twist)[:, None, None, :]
    inner = angles(width, width, width)
    inner_cos, inner_sin = np.cos(inner), np.sin(inner)
    stage_b = np.concatenate(
        [np.concatenate([inner_cos, -inner_sin], axis=1), np.concatenate([inner_sin, inner_cos], axis=1)],
        axis=0,
    )
    back_b = np.concatenate(
        [np.concatenate([inner_cos, inner_sin], axis=1), np.concatenate([-inner_sin, inner_cos], axis=1)],
        axis=0,
    )
    back_a = np.concatenate([np.cos(outer).T, -np.sin(outer).T], axis=1) / total
    as_f32 = lambda a: jnp.asarray(a.astype(np.float32))
    return tuple(as_f32(a) for a in (stage_a, twist_cos, twist_sin, stage_b, back_b, back_a))


def long_mix(stacked):
    blocks, _, _, width = stacked.shape
    stage_a, twist_cos, twist_sin, stage_b, back_b, back_a = dft_tables(blocks, width)
    freq_blocks = 2 * blocks
    outer = jnp.einsum("kp,pscm->kscm", stage_a, stacked, precision=PRECISE)
    outer_re, outer_im = outer[:freq_blocks], outer[freq_blocks:]
    turned_re = outer_re * twist_cos + outer_im * twist_sin
    turned_im = outer_im * twist_cos - outer_re * twist_sin
    spec = jnp.einsum("kscm,mn->kscn", turned_re, stage_b[:width], precision=PRECISE) + jnp.einsum(
        "kscm,mn->kscn", turned_im, stage_b[width:], precision=PRECISE
    )
    spec_re, spec_im = spec[..., :width], spec[..., width:]
    filt_re, sig_re, grad_re = spec_re[:, 0], spec_re[:, 1], spec_re[:, 2]
    filt_im, sig_im, grad_im = spec_im[:, 0], spec_im[:, 1], spec_im[:, 2]
    prod_re = jnp.stack(
        [
            filt_re * sig_re - filt_im * sig_im,
            filt_re * grad_re + filt_im * grad_im,
            sig_re * grad_re + sig_im * grad_im,
        ],
        axis=1,
    )
    prod_im = jnp.stack(
        [
            filt_re * sig_im + filt_im * sig_re,
            filt_re * grad_im - filt_im * grad_re,
            sig_re * grad_im - sig_im * grad_re,
        ],
        axis=1,
    )
    inner = jnp.einsum("kscn,nm->kscm", prod_re, back_b[:width], precision=PRECISE) + jnp.einsum(
        "kscn,nm->kscm", prod_im, back_b[width:], precision=PRECISE
    )
    inner_re, inner_im = inner[..., :width], inner[..., width:]
    back_re = inner_re * twist_cos - inner_im * twist_sin
    back_im = inner_re * twist_sin + inner_im * twist_cos
    both = jnp.concatenate([back_re, back_im], axis=0)
    return jnp.einsum("pk,kscm->pscm", back_a, both, precision=PRECISE)


def shift_back(x, by, lane):
    earlier = jnp.concatenate([jnp.zeros_like(x[:1]), x[:-1]], axis=0)
    return jnp.where(lane < by, jnp.roll(earlier, by, axis=-1), jnp.roll(x, by, axis=-1))


def shift_ahead(x, by, lane):
    later = jnp.concatenate([x[1:], jnp.zeros_like(x[:1])], axis=0)
    width = x.shape[-1]
    return jnp.where(lane >= width - by, jnp.roll(later, -by, axis=-1), jnp.roll(x, -by, axis=-1))


def to_tokens_in_lanes(block, parts):
    rows, cols = block.shape[-2:]
    swapped = jnp.swapaxes(block, -1, -2)
    return swapped.reshape(block.shape[:-2] + (parts, cols // parts, rows))


def from_tokens_in_lanes(block):
    lead = block.shape[:-3]
    parts, sub, rows = block.shape[-3:]
    return jnp.swapaxes(block.reshape(lead + (parts * sub, rows)), -1, -2)


def on_device(layer_input, value_pre, gate_act, key_act, short_taps, long_filter, grad_out):
    n_seq = lax.axis_size("seq")
    n_chan = lax.axis_size("chan")
    me = lax.axis_index("seq")
    tap_count = short_taps.shape[0]
    sub = value_pre.shape[1] // n_seq

    inputs_all = lax.all_gather(layer_input, "seq", axis=0, tiled=True)

    halves = to_tokens_in_lanes(jnp.stack([value_pre, gate_act, key_act, grad_out]), n_seq)
    halves = lax.all_to_all(halves, "seq", split_axis=1, concat_axis=1, tiled=True)
    filt = lax.all_to_all(to_tokens_in_lanes(long_filter, n_seq), "seq", split_axis=0, concat_axis=0, tiled=True)
    value_t = halves[0].astype(F32)
    gate_t = halves[1].astype(F32)
    key_t = halves[2].astype(F32)
    gout_t = halves[3].astype(F32)
    taps = lax.dynamic_slice_in_dim(short_taps, me * sub, sub, axis=1)[:, :, None]
    lane = lax.broadcasted_iota(jnp.int32, value_t.shape, 2)

    value_shifted = [value_t] + [shift_back(value_t, j, lane) for j in range(1, tap_count)]
    conv_val = taps[0] * value_shifted[0]
    for tap_index in range(1, tap_count):
        conv_val = conv_val + taps[tap_index] * value_shifted[tap_index]
    signal = key_t * conv_val
    grad_mix = gout_t * gate_t
    mixed = long_mix(jnp.stack([filt, signal, grad_mix], axis=1))
    mix_out, grad_signal, grad_filter = mixed[:, 0], mixed[:, 1], mixed[:, 2]
    grad_gate = (gout_t * mix_out).astype(BF16)
    grad_key = (grad_signal * conv_val).astype(BF16)
    grad_conv = grad_signal * key_t
    value_sum = taps[0] * grad_conv
    for tap_index in range(1, tap_count):
        value_sum = value_sum + taps[tap_index] * shift_ahead(grad_conv, tap_index, lane)
    grad_value = value_sum.astype(BF16)
    tap_rows = [jnp.sum(grad_conv * value_shifted[j], axis=(0, 2)) for j in range(tap_count)]
    grad_taps = lax.all_gather(jnp.stack(tap_rows, axis=0), "seq", axis=1, tiled=True)

    outs = jnp.stack([grad_gate, grad_key, grad_value])
    outs = from_tokens_in_lanes(lax.all_to_all(outs, "seq", split_axis=1, concat_axis=1, tiled=True))
    grad_filter = from_tokens_in_lanes(
        lax.all_to_all(grad_filter, "seq", split_axis=0, concat_axis=0, tiled=True)
    )

    swap = [(a * n_chan + b, b * n_chan + a) for a in range(n_seq) for b in range(n_chan)]
    value_swapped = lax.ppermute(grad_value, ("seq", "chan"), swap)
    value_cols = lax.all_gather(value_swapped, "chan", axis=0, tiled=False)
    blocks, width = value_t.shape[0], value_t.shape[2]
    inputs_3 = inputs_all.reshape(blocks, width, inputs_all.shape[1])
    grad_proj = jnp.einsum("pmi,cpom->ico", inputs_3, value_cols, preferred_element_type=F32)
    grad_proj = grad_proj.reshape(grad_proj.shape[0], -1)
    return (outs[0], outs[1], outs[2], grad_taps, grad_filter, grad_proj)


def solution(mesh):
    assert mesh.shape["seq"] == mesh.shape["chan"]
    in_specs = (
        P("seq", "chan"),
        P("seq", "chan"),
        P("seq", "chan"),
        P("seq", "chan"),
        P(None, "chan"),
        P("seq", "chan"),
        P("seq", "chan"),
    )
    out_specs = (
        P("seq", "chan"),
        P("seq", "chan"),
        P("seq", "chan"),
        P(None, "chan"),
        P("seq", "chan"),
        P("chan", "seq"),
    )
    return jax.shard_map(
        on_device, mesh=mesh, in_specs=in_specs, out_specs=out_specs, check_vma=False
    )
```

```python
import numpy as np

import jax
import jax.numpy as jnp
from jax import lax
from jax.sharding import PartitionSpec as P

F32 = jnp.float32
BF16 = jnp.bfloat16
PRECISE = lax.Precision.HIGHEST


def angles(rows, cols, period):
    product = np.outer(np.arange(rows), np.arange(cols)) % period
    return product.astype(np.float64) * (2.0 * np.pi / period)


def dft_tables(blocks, width):
    freq_blocks = 2 * blocks
    total = freq_blocks * width
    outer = angles(freq_blocks, blocks, freq_blocks)
    stage_a = np.concatenate([np.cos(outer), -np.sin(outer)], axis=0)
    twist = angles(freq_blocks, width, total)
    twist_cos = np.cos(twist)[:, None, None, :]
    twist_sin = np.sin(twist)[:, None, None, :]
    inner = angles(width, width, width)
    inner_cos, inner_sin = np.cos(inner), np.sin(inner)
    stage_b = np.concatenate(
        [np.concatenate([inner_cos, -inner_sin], axis=1), np.concatenate([inner_sin, inner_cos], axis=1)],
        axis=0,
    )
    back_b = np.concatenate(
        [np.concatenate([inner_cos, inner_sin], axis=1), np.concatenate([-inner_sin, inner_cos], axis=1)],
        axis=0,
    )
    back_a = np.concatenate([np.cos(outer).T, -np.sin(outer).T], axis=1) / total
    as_f32 = lambda a: jnp.asarray(a.astype(np.float32))
    return tuple(as_f32(a) for a in (stage_a, twist_cos, twist_sin, stage_b, back_b, back_a))


def long_mix(stacked):
    blocks, _, _, width = stacked.shape
    stage_a, twist_cos, twist_sin, stage_b, back_b, back_a = dft_tables(blocks, width)
    freq_blocks = 2 * blocks
    outer = jnp.einsum("kp,pscm->kscm", stage_a, stacked, precision=PRECISE)
    outer_re, outer_im = outer[:freq_blocks], outer[freq_blocks:]
    turned_re = outer_re * twist_cos + outer_im * twist_sin
    turned_im = outer_im * twist_cos - outer_re * twist_sin
    spec = jnp.einsum("kscm,mn->kscn", turned_re, stage_b[:width], precision=PRECISE) + jnp.einsum(
        "kscm,mn->kscn", turned_im, stage_b[width:], precision=PRECISE
    )
    spec_re, spec_im = spec[..., :width], spec[..., width:]
    filt_re, sig_re, grad_re = spec_re[:, 0], spec_re[:, 1], spec_re[:, 2]
    filt_im, sig_im, grad_im = spec_im[:, 0], spec_im[:, 1], spec_im[:, 2]
    prod_re = jnp.stack(
        [
            filt_re * sig_re - filt_im * sig_im,
            filt_re * grad_re + filt_im * grad_im,
            sig_re * grad_re + sig_im * grad_im,
        ],
        axis=1,
    )
    prod_im = jnp.stack(
        [
            filt_re * sig_im + filt_im * sig_re,
            filt_re * grad_im - filt_im * grad_re,
            sig_re * grad_im - sig_im * grad_re,
        ],
        axis=1,
    )
    inner = jnp.einsum("kscn,nm->kscm", prod_re, back_b[:width], precision=PRECISE) + jnp.einsum(
        "kscn,nm->kscm", prod_im, back_b[width:], precision=PRECISE
    )
    inner_re, inner_im = inner[..., :width], inner[..., width:]
    back_re = inner_re * twist_cos - inner_im * twist_sin
    back_im = inner_re * twist_sin + inner_im * twist_cos
    both = jnp.concatenate([back_re, back_im], axis=0)
    return jnp.einsum("pk,kscm->pscm", back_a, both, precision=PRECISE)


def shift_back(x, by, lane):
    earlier = jnp.concatenate([jnp.zeros_like(x[:1]), x[:-1]], axis=0)
    return jnp.where(lane < by, jnp.roll(earlier, by, axis=-1), jnp.roll(x, by, axis=-1))


def shift_ahead(x, by, lane):
    later = jnp.concatenate([x[1:], jnp.zeros_like(x[:1])], axis=0)
    width = x.shape[-1]
    return jnp.where(lane >= width - by, jnp.roll(later, -by, axis=-1), jnp.roll(x, -by, axis=-1))


def to_tokens_in_lanes(block, parts):
    rows, cols = block.shape[-2:]
    swapped = jnp.swapaxes(block, -1, -2)
    return swapped.reshape(block.shape[:-2] + (parts, cols // parts, rows))


def from_tokens_in_lanes(block):
    lead = block.shape[:-3]
    parts, sub, rows = block.shape[-3:]
    return jnp.swapaxes(block.reshape(lead + (parts * sub, rows)), -1, -2)


def split_words(x):
    rounded = lax.reduce_precision(x, exponent_bits=8, mantissa_bits=7)
    return rounded.astype(BF16), (x - rounded).astype(BF16)


def join_words(high, low):
    return high.astype(F32) + low.astype(F32)


def on_device(layer_input, value_pre, gate_act, key_act, short_taps, long_filter, grad_out):
    n_seq = lax.axis_size("seq")
    n_chan = lax.axis_size("chan")
    me = lax.axis_index("seq")
    tap_count = short_taps.shape[0]
    sub = value_pre.shape[1] // n_seq

    inputs_all = lax.all_gather(layer_input, "seq", axis=0, tiled=True)

    filt_high, filt_low = split_words(long_filter)
    sent = to_tokens_in_lanes(jnp.stack([value_pre, gate_act, key_act, grad_out, filt_high, filt_low]), n_seq)
    got = lax.all_to_all(sent, "seq", split_axis=1, concat_axis=1, tiled=True)
    value_t = got[0].astype(F32)
    gate_t = got[1].astype(F32)
    key_t = got[2].astype(F32)
    gout_t = got[3].astype(F32)
    filt = join_words(got[4], got[5])
    taps = lax.dynamic_slice_in_dim(short_taps, me * sub, sub, axis=1)[:, :, None]
    lane = lax.broadcasted_iota(jnp.int32, value_t.shape, 2)

    value_shifted = [value_t] + [shift_back(value_t, j, lane) for j in range(1, tap_count)]
    conv_val = taps[0] * value_shifted[0]
    for tap_index in range(1, tap_count):
        conv_val = conv_val + taps[tap_index] * value_shifted[tap_index]
    signal = key_t * conv_val
    grad_mix = gout_t * gate_t
    mixed = long_mix(jnp.stack([filt, signal, grad_mix], axis=1))
    mix_out, grad_signal, grad_filter = mixed[:, 0], mixed[:, 1], mixed[:, 2]
    grad_gate = (gout_t * mix_out).astype(BF16)
    grad_key = (grad_signal * conv_val).astype(BF16)
    grad_conv = grad_signal * key_t
    value_sum = taps[0] * grad_conv
    for tap_index in range(1, tap_count):
        value_sum = value_sum + taps[tap_index] * shift_ahead(grad_conv, tap_index, lane)
    grad_value = value_sum.astype(BF16)

    swap = [(a * n_chan + b, b * n_chan + a) for a in range(n_seq) for b in range(n_chan)]
    value_swapped = lax.ppermute(grad_value, ("seq", "chan"), swap)
    value_cols = lax.all_to_all(
        jnp.broadcast_to(value_swapped[None], (n_chan,) + value_swapped.shape),
        "chan", split_axis=0, concat_axis=0, tiled=True,
    )

    tap_rows = jnp.stack([jnp.sum(grad_conv * value_shifted[j], axis=(0, 2)) for j in range(tap_count)])
    taps_high, taps_low = split_words(tap_rows)
    width = value_t.shape[2]
    taps_slab = jnp.pad(jnp.concatenate([taps_high, taps_low], axis=0).T, ((0, 0), (0, width - 2 * tap_count)))
    taps_slab = jnp.broadcast_to(taps_slab[None], value_t.shape)
    gf_high, gf_low = split_words(grad_filter)
    outs = jnp.stack([grad_gate, grad_key, grad_value, gf_high, gf_low, taps_slab])
    outs = lax.all_to_all(outs, "seq", split_axis=1, concat_axis=1, tiled=True)
    taps_got = outs[5, :, :, : 2 * tap_count]
    grad_taps = join_words(taps_got[..., :tap_count], taps_got[..., tap_count:])
    grad_taps = jnp.transpose(grad_taps, (2, 0, 1)).reshape(tap_count, -1)
    outs = from_tokens_in_lanes(outs[:5])
    grad_filter = join_words(outs[3], outs[4])

    blocks = value_t.shape[0]
    inputs_3 = inputs_all.reshape(blocks, width, inputs_all.shape[1])
    grad_proj = jnp.einsum("pmi,cpom->ico", inputs_3, value_cols, preferred_element_type=F32)
    grad_proj = grad_proj.reshape(grad_proj.shape[0], -1)
    return (outs[0], outs[1], outs[2], grad_taps, grad_filter, grad_proj)


def solution(mesh):
    assert mesh.shape["seq"] == mesh.shape["chan"]
    in_specs = (
        P("seq", "chan"),
        P("seq", "chan"),
        P("seq", "chan"),
        P("seq", "chan"),
        P(None, "chan"),
        P("seq", "chan"),
        P("seq", "chan"),
    )
    out_specs = (
        P("seq", "chan"),
        P("seq", "chan"),
        P("seq", "chan"),
        P(None, "chan"),
        P("seq", "chan"),
        P("chan", "seq"),
    )
    return jax.shard_map(
        on_device, mesh=mesh, in_specs=in_specs, out_specs=out_specs, check_vma=False
    )
```

```python
import numpy as np

import jax
import jax.numpy as jnp
from jax import lax
from jax.sharding import PartitionSpec as P

F32 = jnp.float32
BF16 = jnp.bfloat16
PRECISE = lax.Precision.HIGHEST


def angles(rows, cols, period):
    product = np.outer(np.arange(rows), np.arange(cols)) % period
    return product.astype(np.float64) * (2.0 * np.pi / period)


def dft_tables(blocks, width):
    freq_blocks = 2 * blocks
    total = freq_blocks * width
    outer = angles(freq_blocks, blocks, freq_blocks)
    stage_a = np.concatenate([np.cos(outer), -np.sin(outer)], axis=0)
    twist = angles(freq_blocks, width, total)
    twist_cos = np.cos(twist)[:, None, None, :]
    twist_sin = np.sin(twist)[:, None, None, :]
    inner = angles(width, width, width)
    inner_cos, inner_sin = np.cos(inner), np.sin(inner)
    stage_b = np.concatenate(
        [np.concatenate([inner_cos, -inner_sin], axis=1), np.concatenate([inner_sin, inner_cos], axis=1)],
        axis=0,
    )
    back_b = np.concatenate(
        [np.concatenate([inner_cos, inner_sin], axis=1), np.concatenate([-inner_sin, inner_cos], axis=1)],
        axis=0,
    )
    back_a = np.concatenate([np.cos(outer).T, -np.sin(outer).T], axis=1) / total
    as_f32 = lambda a: jnp.asarray(a.astype(np.float32))
    return tuple(as_f32(a) for a in (stage_a, twist_cos, twist_sin, stage_b, back_b, back_a))


def spectra(stacked, tables):
    stage_a, twist_cos, twist_sin, stage_b, _, _ = tables
    freq_blocks = 2 * stacked.shape[0]
    width = stacked.shape[-1]
    outer = jnp.einsum("kp,pscm->kscm", stage_a, stacked, precision=PRECISE)
    outer_re, outer_im = outer[:freq_blocks], outer[freq_blocks:]
    turned_re = outer_re * twist_cos + outer_im * twist_sin
    turned_im = outer_im * twist_cos - outer_re * twist_sin
    spec = jnp.einsum("kscm,mn->kscn", turned_re, stage_b[:width], precision=PRECISE) + jnp.einsum(
        "kscm,mn->kscn", turned_im, stage_b[width:], precision=PRECISE
    )
    return spec[..., :width], spec[..., width:]


def signals_back(prod_re, prod_im, tables):
    _, twist_cos, twist_sin, _, back_b, back_a = tables
    width = prod_re.shape[-1]
    inner = jnp.einsum("kscn,nm->kscm", prod_re, back_b[:width], precision=PRECISE) + jnp.einsum(
        "kscn,nm->kscm", prod_im, back_b[width:], precision=PRECISE
    )
    inner_re, inner_im = inner[..., :width], inner[..., width:]
    back_re = inner_re * twist_cos - inner_im * twist_sin
    back_im = inner_re * twist_sin + inner_im * twist_cos
    both = jnp.concatenate([back_re, back_im], axis=0)
    return jnp.einsum("pk,kscm->pscm", back_a, both, precision=PRECISE)


def shift_back(x, by, lane):
    earlier = jnp.concatenate([jnp.zeros_like(x[:1]), x[:-1]], axis=0)
    return jnp.where(lane < by, jnp.roll(earlier, by, axis=-1), jnp.roll(x, by, axis=-1))


def shift_ahead(x, by, lane):
    later = jnp.concatenate([x[1:], jnp.zeros_like(x[:1])], axis=0)
    width = x.shape[-1]
    return jnp.where(lane >= width - by, jnp.roll(later, -by, axis=-1), jnp.roll(x, -by, axis=-1))


def to_tokens_in_lanes(block, parts):
    rows, cols = block.shape[-2:]
    swapped = jnp.swapaxes(block, -1, -2)
    return swapped.reshape(block.shape[:-2] + (parts, cols // parts, rows))


def from_tokens_in_lanes(block):
    lead = block.shape[:-3]
    parts, sub, rows = block.shape[-3:]
    return jnp.swapaxes(block.reshape(lead + (parts * sub, rows)), -1, -2)


def split_words(x):
    rounded = lax.reduce_precision(x, exponent_bits=8, mantissa_bits=7)
    return rounded.astype(BF16), (x - rounded).astype(BF16)


def join_words(high, low):
    return high.astype(F32) + low.astype(F32)


def on_device(layer_input, value_pre, gate_act, key_act, short_taps, long_filter, grad_out):
    n_seq = lax.axis_size("seq")
    n_chan = lax.axis_size("chan")
    me = lax.axis_index("seq")
    tap_count = short_taps.shape[0]
    sub = value_pre.shape[1] // n_seq

    inputs_all = lax.all_gather(layer_input, "seq", axis=0, tiled=True)

    filt_high, filt_low = split_words(long_filter)
    sent = to_tokens_in_lanes(jnp.stack([value_pre, gate_act, key_act, grad_out, filt_high, filt_low]), n_seq)
    got = lax.all_to_all(sent, "seq", split_axis=1, concat_axis=1, tiled=True)
    value_t = got[0].astype(F32)
    gate_t = got[1].astype(F32)
    key_t = got[2].astype(F32)
    gout_t = got[3].astype(F32)
    filt = join_words(got[4], got[5])
    taps = lax.dynamic_slice_in_dim(short_taps, me * sub, sub, axis=1)[:, :, None]
    lane = lax.broadcasted_iota(jnp.int32, value_t.shape, 2)

    value_shifted = [value_t] + [shift_back(value_t, j, lane) for j in range(1, tap_count)]
    conv_val = taps[0] * value_shifted[0]
    for tap_index in range(1, tap_count):
        conv_val = conv_val + taps[tap_index] * value_shifted[tap_index]
    signal = key_t * conv_val
    grad_mix = gout_t * gate_t
    tables = dft_tables(value_t.shape[0], value_t.shape[2])
    fg_re, fg_im = spectra(jnp.stack([filt, grad_mix], axis=1), tables)
    filt_re, grad_re = fg_re[:, 0:1], fg_re[:, 1:2]
    filt_im, grad_im = fg_im[:, 0:1], fg_im[:, 1:2]
    grad_signal = signals_back(
        filt_re * grad_re + filt_im * grad_im, filt_re * grad_im - filt_im * grad_re, tables
    )[:, 0]
    grad_key = (grad_signal * conv_val).astype(BF16)
    grad_conv = grad_signal * key_t
    value_sum = taps[0] * grad_conv
    for tap_index in range(1, tap_count):
        value_sum = value_sum + taps[tap_index] * shift_ahead(grad_conv, tap_index, lane)
    grad_value = value_sum.astype(BF16)

    received = []
    for k in range(n_seq):
        pairs = [(a * n_chan + b, b * n_chan + (a - k) % n_seq) for a in range(n_seq) for b in range(n_chan)]
        received.append(lax.ppermute(grad_value, ("seq", "chan"), pairs))
    received = jnp.stack(received)

    sig_re, sig_im = spectra(signal[:, None], tables)
    prod_re = jnp.concatenate(
        [filt_re * sig_re - filt_im * sig_im, sig_re * grad_re + sig_im * grad_im], axis=1
    )
    prod_im = jnp.concatenate(
        [filt_re * sig_im + filt_im * sig_re, sig_re * grad_im - sig_im * grad_re], axis=1
    )
    mixed = signals_back(prod_re, prod_im, tables)
    mix_out, grad_filter = mixed[:, 0], mixed[:, 1]
    grad_gate = (gout_t * mix_out).astype(BF16)

    tap_rows = jnp.stack([jnp.sum(grad_conv * value_shifted[j], axis=(0, 2)) for j in range(tap_count)])
    taps_high, taps_low = split_words(tap_rows)
    width = value_t.shape[2]
    taps_slab = jnp.pad(jnp.concatenate([taps_high, taps_low], axis=0).T, ((0, 0), (0, width - 2 * tap_count)))
    taps_slab = jnp.broadcast_to(taps_slab[None], value_t.shape)
    gf_high, gf_low = split_words(grad_filter)
    outs = jnp.stack([grad_gate, grad_key, grad_value, gf_high, gf_low, taps_slab])
    outs = lax.all_to_all(outs, "seq", split_axis=1, concat_axis=1, tiled=True)
    taps_got = outs[5, :, :, : 2 * tap_count]
    grad_taps = join_words(taps_got[..., :tap_count], taps_got[..., tap_count:])
    grad_taps = jnp.transpose(grad_taps, (2, 0, 1)).reshape(tap_count, -1)
    outs = from_tokens_in_lanes(outs[:5])
    grad_filter = join_words(outs[3], outs[4])

    blocks = value_t.shape[0]
    inputs_3 = inputs_all.reshape(blocks, width, inputs_all.shape[1])
    grad_proj = jnp.einsum("pmi,kpom->iko", inputs_3, received, preferred_element_type=F32)
    grad_proj = jnp.roll(grad_proj, lax.axis_index("chan"), axis=1)
    grad_proj = grad_proj.reshape(grad_proj.shape[0], -1)
    return (outs[0], outs[1], outs[2], grad_taps, grad_filter, grad_proj)


def solution(mesh):
    assert mesh.shape["seq"] == mesh.shape["chan"]
    in_specs = (
        P("seq", "chan"),
        P("seq", "chan"),
        P("seq", "chan"),
        P("seq", "chan"),
        P(None, "chan"),
        P("seq", "chan"),
        P("seq", "chan"),
    )
    out_specs = (
        P("seq", "chan"),
        P("seq", "chan"),
        P("seq", "chan"),
        P(None, "chan"),
        P("seq", "chan"),
        P("chan", "seq"),
    )
    return jax.shard_map(
        on_device, mesh=mesh, in_specs=in_specs, out_specs=out_specs, check_vma=False
    )
```

```python
import numpy as np

import jax
import jax.numpy as jnp
from jax import lax
from jax.sharding import PartitionSpec as P

F32 = jnp.float32
BF16 = jnp.bfloat16
PRECISE = lax.Precision.HIGHEST


def angles(rows, cols, period):
    product = np.outer(np.arange(rows), np.arange(cols)) % period
    return product.astype(np.float64) * (2.0 * np.pi / period)


def dft_tables(blocks, width):
    freq_blocks = 2 * blocks
    total = freq_blocks * width
    outer = angles(freq_blocks, blocks, freq_blocks)
    stage_a = np.concatenate([np.cos(outer), -np.sin(outer)], axis=0)
    twist = angles(freq_blocks, width, total)
    twist_cos = np.cos(twist)[:, None, None, :]
    twist_sin = np.sin(twist)[:, None, None, :]
    inner = angles(width, width, width)
    inner_cos, inner_sin = np.cos(inner), np.sin(inner)
    stage_b = np.concatenate(
        [np.concatenate([inner_cos, -inner_sin], axis=1), np.concatenate([inner_sin, inner_cos], axis=1)],
        axis=0,
    )
    back_b = np.concatenate(
        [np.concatenate([inner_cos, inner_sin], axis=1), np.concatenate([-inner_sin, inner_cos], axis=1)],
        axis=0,
    )
    back_a = np.concatenate([np.cos(outer).T, -np.sin(outer).T], axis=1) / total
    as_f32 = lambda a: jnp.asarray(a.astype(np.float32))
    return tuple(as_f32(a) for a in (stage_a, twist_cos, twist_sin, stage_b, back_b, back_a))


def spectra(stacked, tables):
    stage_a, twist_cos, twist_sin, stage_b, _, _ = tables
    freq_blocks = 2 * stacked.shape[0]
    width = stacked.shape[-1]
    outer = jnp.einsum("kp,pscm->kscm", stage_a, stacked, precision=PRECISE)
    outer_re, outer_im = outer[:freq_blocks], outer[freq_blocks:]
    turned_re = outer_re * twist_cos + outer_im * twist_sin
    turned_im = outer_im * twist_cos - outer_re * twist_sin
    spec = jnp.einsum("kscm,mn->kscn", turned_re, stage_b[:width], precision=PRECISE) + jnp.einsum(
        "kscm,mn->kscn", turned_im, stage_b[width:], precision=PRECISE
    )
    return spec[..., :width], spec[..., width:]


def signals_back(prod_re, prod_im, tables):
    _, twist_cos, twist_sin, _, back_b, back_a = tables
    width = prod_re.shape[-1]
    inner = jnp.einsum("kscn,nm->kscm", prod_re, back_b[:width], precision=PRECISE) + jnp.einsum(
        "kscn,nm->kscm", prod_im, back_b[width:], precision=PRECISE
    )
    inner_re, inner_im = inner[..., :width], inner[..., width:]
    back_re = inner_re * twist_cos - inner_im * twist_sin
    back_im = inner_re * twist_sin + inner_im * twist_cos
    both = jnp.concatenate([back_re, back_im], axis=0)
    return jnp.einsum("pk,kscm->pscm", back_a, both, precision=PRECISE)


def shift_back(x, by, lane):
    earlier = jnp.concatenate([jnp.zeros_like(x[:1]), x[:-1]], axis=0)
    return jnp.where(lane < by, jnp.roll(earlier, by, axis=-1), jnp.roll(x, by, axis=-1))


def shift_ahead(x, by, lane):
    later = jnp.concatenate([x[1:], jnp.zeros_like(x[:1])], axis=0)
    width = x.shape[-1]
    return jnp.where(lane >= width - by, jnp.roll(later, -by, axis=-1), jnp.roll(x, -by, axis=-1))


def to_tokens_in_lanes(block, parts):
    rows, cols = block.shape[-2:]
    swapped = jnp.swapaxes(block, -1, -2)
    return swapped.reshape(block.shape[:-2] + (parts, cols // parts, rows))


def from_tokens_in_lanes(block):
    lead = block.shape[:-3]
    parts, sub, rows = block.shape[-3:]
    return jnp.swapaxes(block.reshape(lead + (parts * sub, rows)), -1, -2)


def split_words(x):
    rounded = lax.reduce_precision(x, exponent_bits=8, mantissa_bits=7)
    return rounded.astype(BF16), (x - rounded).astype(BF16)


def join_words(high, low):
    return high.astype(F32) + low.astype(F32)


def on_device(layer_input, value_pre, gate_act, key_act, short_taps, long_filter, grad_out):
    n_seq = lax.axis_size("seq")
    n_chan = lax.axis_size("chan")
    me = lax.axis_index("seq")
    tap_count = short_taps.shape[0]
    sub = value_pre.shape[1] // n_seq

    filt_high, filt_low = split_words(long_filter)
    sent = to_tokens_in_lanes(jnp.stack([value_pre, gate_act, key_act, grad_out, filt_high, filt_low]), n_seq)
    got = lax.all_to_all(sent, "seq", split_axis=1, concat_axis=1, tiled=True)
    value_t = got[0].astype(F32)
    gate_t = got[1].astype(F32)
    key_t = got[2].astype(F32)
    gout_t = got[3].astype(F32)
    filt = join_words(got[4], got[5])
    taps = lax.dynamic_slice_in_dim(short_taps, me * sub, sub, axis=1)[:, :, None]
    lane = lax.broadcasted_iota(jnp.int32, value_t.shape, 2)

    value_shifted = [value_t] + [shift_back(value_t, j, lane) for j in range(1, tap_count)]
    conv_val = taps[0] * value_shifted[0]
    for tap_index in range(1, tap_count):
        conv_val = conv_val + taps[tap_index] * value_shifted[tap_index]
    signal = key_t * conv_val
    grad_mix = gout_t * gate_t
    tables = dft_tables(value_t.shape[0], value_t.shape[2])
    fg_re, fg_im = spectra(jnp.stack([filt, grad_mix], axis=1), tables)
    filt_re, grad_re = fg_re[:, 0:1], fg_re[:, 1:2]
    filt_im, grad_im = fg_im[:, 0:1], fg_im[:, 1:2]
    grad_signal = signals_back(
        filt_re * grad_re + filt_im * grad_im, filt_re * grad_im - filt_im * grad_re, tables
    )[:, 0]
    grad_key = (grad_signal * conv_val).astype(BF16)
    grad_conv = grad_signal * key_t
    value_sum = taps[0] * grad_conv
    for tap_index in range(1, tap_count):
        value_sum = value_sum + taps[tap_index] * shift_ahead(grad_conv, tap_index, lane)
    grad_value = value_sum.astype(BF16)

    swap = [(a * n_chan + b, b * n_chan + a) for a in range(n_seq) for b in range(n_chan)]
    value_swapped = lax.ppermute(grad_value, ("seq", "chan"), swap)
    value_cols = lax.all_gather(value_swapped, "chan", axis=0, tiled=False)
    late_input, _ = lax.optimization_barrier((layer_input, value_swapped))
    inputs_all = lax.all_to_all(
        jnp.broadcast_to(late_input[None], (n_seq,) + late_input.shape),
        "seq", split_axis=0, concat_axis=0, tiled=True,
    ).reshape(-1, late_input.shape[1])

    sig_re, sig_im = spectra(signal[:, None], tables)
    prod_re = jnp.concatenate(
        [filt_re * sig_re - filt_im * sig_im, sig_re * grad_re + sig_im * grad_im], axis=1
    )
    prod_im = jnp.concatenate(
        [filt_re * sig_im + filt_im * sig_re, sig_re * grad_im - sig_im * grad_re], axis=1
    )
    mixed = signals_back(prod_re, prod_im, tables)
    mix_out, grad_filter = mixed[:, 0], mixed[:, 1]
    grad_gate = (gout_t * mix_out).astype(BF16)

    tap_rows = jnp.stack([jnp.sum(grad_conv * value_shifted[j], axis=(0, 2)) for j in range(tap_count)])
    taps_high, taps_low = split_words(tap_rows)
    width = value_t.shape[2]
    taps_slab = jnp.pad(jnp.concatenate([taps_high, taps_low], axis=0).T, ((0, 0), (0, width - 2 * tap_count)))
    taps_slab = jnp.broadcast_to(taps_slab[None], value_t.shape)
    gf_high, gf_low = split_words(grad_filter)
    outs = jnp.stack([grad_gate, grad_key, grad_value, gf_high, gf_low, taps_slab])
    outs = lax.all_to_all(outs, "seq", split_axis=1, concat_axis=1, tiled=True)
    taps_got = outs[5, :, :, : 2 * tap_count]
    grad_taps = join_words(taps_got[..., :tap_count], taps_got[..., tap_count:])
    grad_taps = jnp.transpose(grad_taps, (2, 0, 1)).reshape(tap_count, -1)
    outs = from_tokens_in_lanes(outs[:5])
    grad_filter = join_words(outs[3], outs[4])

    blocks = value_t.shape[0]
    inputs_3 = inputs_all.reshape(blocks, width, inputs_all.shape[1])
    grad_proj = jnp.einsum("pmi,cpom->ico", inputs_3, value_cols, preferred_element_type=F32)
    grad_proj = grad_proj.reshape(grad_proj.shape[0], -1)
    return (outs[0], outs[1], outs[2], grad_taps, grad_filter, grad_proj)


def solution(mesh):
    assert mesh.shape["seq"] == mesh.shape["chan"]
    in_specs = (
        P("seq", "chan"),
        P("seq", "chan"),
        P("seq", "chan"),
        P("seq", "chan"),
        P(None, "chan"),
        P("seq", "chan"),
        P("seq", "chan"),
    )
    out_specs = (
        P("seq", "chan"),
        P("seq", "chan"),
        P("seq", "chan"),
        P(None, "chan"),
        P("seq", "chan"),
        P("chan", "seq"),
    )
    return jax.shard_map(
        on_device, mesh=mesh, in_specs=in_specs, out_specs=out_specs, check_vma=False
    )
```

```python
import numpy as np

import jax
import jax.numpy as jnp
from jax import lax
from jax.sharding import PartitionSpec as P

F32 = jnp.float32
BF16 = jnp.bfloat16
PRECISE = lax.Precision.HIGHEST


def angles(rows, cols, period):
    product = np.outer(np.arange(rows), np.arange(cols)) % period
    return product.astype(np.float64) * (2.0 * np.pi / period)


def dft_tables(blocks, width):
    freq_blocks = 2 * blocks
    total = freq_blocks * width
    outer = angles(freq_blocks, blocks, freq_blocks)
    stage_a = np.concatenate([np.cos(outer), -np.sin(outer)], axis=0)
    twist = angles(freq_blocks, width, total)
    twist_cos = np.cos(twist)[:, None, None, :]
    twist_sin = np.sin(twist)[:, None, None, :]
    inner = angles(width, width, width)
    inner_cos, inner_sin = np.cos(inner), np.sin(inner)
    stage_b = np.concatenate(
        [np.concatenate([inner_cos, -inner_sin], axis=1), np.concatenate([inner_sin, inner_cos], axis=1)],
        axis=0,
    )
    back_b = np.concatenate(
        [np.concatenate([inner_cos, inner_sin], axis=1), np.concatenate([-inner_sin, inner_cos], axis=1)],
        axis=0,
    )
    back_a = np.concatenate([np.cos(outer).T, -np.sin(outer).T], axis=1) / total
    as_f32 = lambda a: jnp.asarray(a.astype(np.float32))
    return tuple(as_f32(a) for a in (stage_a, twist_cos, twist_sin, stage_b, back_b, back_a))


def spectra(stacked, tables):
    stage_a, twist_cos, twist_sin, stage_b, _, _ = tables
    freq_blocks = 2 * stacked.shape[0]
    width = stacked.shape[-1]
    outer = jnp.einsum("kp,pscm->kscm", stage_a, stacked, precision=PRECISE)
    outer_re, outer_im = outer[:freq_blocks], outer[freq_blocks:]
    turned_re = outer_re * twist_cos + outer_im * twist_sin
    turned_im = outer_im * twist_cos - outer_re * twist_sin
    spec = jnp.einsum("kscm,mn->kscn", turned_re, stage_b[:width], precision=PRECISE) + jnp.einsum(
        "kscm,mn->kscn", turned_im, stage_b[width:], precision=PRECISE
    )
    return spec[..., :width], spec[..., width:]


def signals_back(prod_re, prod_im, tables):
    _, twist_cos, twist_sin, _, back_b, back_a = tables
    width = prod_re.shape[-1]
    inner = jnp.einsum("kscn,nm->kscm", prod_re, back_b[:width], precision=PRECISE) + jnp.einsum(
        "kscn,nm->kscm", prod_im, back_b[width:], precision=PRECISE
    )
    inner_re, inner_im = inner[..., :width], inner[..., width:]
    back_re = inner_re * twist_cos - inner_im * twist_sin
    back_im = inner_re * twist_sin + inner_im * twist_cos
    both = jnp.concatenate([back_re, back_im], axis=0)
    return jnp.einsum("pk,kscm->pscm", back_a, both, precision=PRECISE)


def shift_back(x, by, lane):
    earlier = jnp.concatenate([jnp.zeros_like(x[:1]), x[:-1]], axis=0)
    return jnp.where(lane < by, jnp.roll(earlier, by, axis=-1), jnp.roll(x, by, axis=-1))


def shift_ahead(x, by, lane):
    later = jnp.concatenate([x[1:], jnp.zeros_like(x[:1])], axis=0)
    width = x.shape[-1]
    return jnp.where(lane >= width - by, jnp.roll(later, -by, axis=-1), jnp.roll(x, -by, axis=-1))


def to_tokens_in_lanes(block, parts):
    rows, cols = block.shape[-2:]
    swapped = jnp.swapaxes(block, -1, -2)
    return swapped.reshape(block.shape[:-2] + (parts, cols // parts, rows))


def from_tokens_in_lanes(block):
    lead = block.shape[:-3]
    parts, sub, rows = block.shape[-3:]
    return jnp.swapaxes(block.reshape(lead + (parts * sub, rows)), -1, -2)


def split_words(x):
    rounded = lax.reduce_precision(x, exponent_bits=8, mantissa_bits=7)
    return rounded.astype(BF16), (x - rounded).astype(BF16)


def join_words(high, low):
    return high.astype(F32) + low.astype(F32)


def on_device(layer_input, value_pre, gate_act, key_act, short_taps, long_filter, grad_out):
    n_seq = lax.axis_size("seq")
    n_chan = lax.axis_size("chan")
    me = lax.axis_index("seq")
    tap_count = short_taps.shape[0]
    sub = value_pre.shape[1] // n_seq

    inputs_all = lax.all_gather(layer_input, "seq", axis=0, tiled=True)

    filt_high, filt_low = split_words(long_filter)
    sent = to_tokens_in_lanes(jnp.stack([value_pre, gate_act, key_act, grad_out, filt_high, filt_low]), n_seq)
    got = lax.all_to_all(sent, "seq", split_axis=1, concat_axis=1, tiled=True)
    value_t = got[0].astype(F32)
    gate_t = got[1].astype(F32)
    key_t = got[2].astype(F32)
    gout_t = got[3].astype(F32)
    filt = join_words(got[4], got[5])
    taps = lax.dynamic_slice_in_dim(short_taps, me * sub, sub, axis=1)[:, :, None]
    lane = lax.broadcasted_iota(jnp.int32, value_t.shape, 2)

    value_shifted = [value_t] + [shift_back(value_t, j, lane) for j in range(1, tap_count)]
    conv_val = taps[0] * value_shifted[0]
    for tap_index in range(1, tap_count):
        conv_val = conv_val + taps[tap_index] * value_shifted[tap_index]
    signal = key_t * conv_val
    grad_mix = gout_t * gate_t
    tables = dft_tables(value_t.shape[0], value_t.shape[2])
    fg_re, fg_im = spectra(jnp.stack([filt, grad_mix], axis=1), tables)
    filt_re, grad_re = fg_re[:, 0:1], fg_re[:, 1:2]
    filt_im, grad_im = fg_im[:, 0:1], fg_im[:, 1:2]
    grad_signal = signals_back(
        filt_re * grad_re + filt_im * grad_im, filt_re * grad_im - filt_im * grad_re, tables
    )[:, 0]
    grad_key = (grad_signal * conv_val).astype(BF16)
    grad_conv = grad_signal * key_t
    value_sum = taps[0] * grad_conv
    for tap_index in range(1, tap_count):
        value_sum = value_sum + taps[tap_index] * shift_ahead(grad_conv, tap_index, lane)
    grad_value = value_sum.astype(BF16)

    swap = [(a * n_chan + b, b * n_chan + a) for a in range(n_seq) for b in range(n_chan)]
    value_swapped = lax.ppermute(grad_value, ("seq", "chan"), swap)
    value_cols = lax.all_gather(value_swapped, "chan", axis=0, tiled=False)

    sig_re, sig_im = spectra(signal[:, None], tables)
    prod_re = jnp.concatenate(
        [filt_re * sig_re - filt_im * sig_im, sig_re * grad_re + sig_im * grad_im], axis=1
    )
    prod_im = jnp.concatenate(
        [filt_re * sig_im + filt_im * sig_re, sig_re * grad_im - sig_im * grad_re], axis=1
    )
    mixed = signals_back(prod_re, prod_im, tables)
    mix_out, grad_filter = mixed[:, 0], mixed[:, 1]
    grad_gate = (gout_t * mix_out).astype(BF16)

    tap_rows = jnp.stack([jnp.sum(grad_conv * value_shifted[j], axis=(0, 2)) for j in range(tap_count)])
    taps_high, taps_low = split_words(tap_rows)
    width = value_t.shape[2]
    taps_slab = jnp.pad(jnp.concatenate([taps_high, taps_low], axis=0).T, ((0, 0), (0, width - 2 * tap_count)))
    taps_slab = jnp.broadcast_to(taps_slab[None], value_t.shape)
    gf_high, gf_low = split_words(grad_filter)
    outs = jnp.stack([grad_gate, grad_key, grad_value, gf_high, gf_low, taps_slab])
    outs = lax.all_to_all(outs, "seq", split_axis=1, concat_axis=1, tiled=True)
    taps_got = outs[5, :, :, : 2 * tap_count]
    grad_taps = join_words(taps_got[..., :tap_count], taps_got[..., tap_count:])
    grad_taps = jnp.transpose(grad_taps, (2, 0, 1)).reshape(tap_count, -1)
    outs = from_tokens_in_lanes(outs[:5])
    grad_filter = join_words(outs[3], outs[4])

    blocks = value_t.shape[0]
    inputs_3 = inputs_all.reshape(blocks, width, inputs_all.shape[1])
    grad_proj = jnp.einsum("pmi,cpom->ico", inputs_3, value_cols, preferred_element_type=F32)
    grad_proj = grad_proj.reshape(grad_proj.shape[0], -1)
    return (outs[0], outs[1], outs[2], grad_taps, grad_filter, grad_proj)


def solution(mesh):
    assert mesh.shape["seq"] == mesh.shape["chan"]
    in_specs = (
        P("seq", "chan"),
        P("seq", "chan"),
        P("seq", "chan"),
        P("seq", "chan"),
        P(None, "chan"),
        P("seq", "chan"),
        P("seq", "chan"),
    )
    out_specs = (
        P("seq", "chan"),
        P("seq", "chan"),
        P("seq", "chan"),
        P(None, "chan"),
        P("seq", "chan"),
        P("chan", "seq"),
    )
    return jax.shard_map(
        on_device, mesh=mesh, in_specs=in_specs, out_specs=out_specs, check_vma=False
    )
```

```python
import numpy as np

import jax
import jax.numpy as jnp
from jax import lax
from jax.sharding import PartitionSpec as P


F32 = jnp.float32
BF16 = jnp.bfloat16
PRECISE = lax.Precision.HIGHEST


def angles(rows, cols, period):
    product = np.outer(np.arange(rows), np.arange(cols)) % period
    return product.astype(np.float64) * (2.0 * np.pi / period)


def dft_tables(blocks, width):
    freq_blocks = 2 * blocks
    total = freq_blocks * width
    outer = angles(freq_blocks, blocks, freq_blocks)
    stage_a = np.concatenate([np.cos(outer), -np.sin(outer)], axis=0)
    twist = angles(freq_blocks, width, total)
    twist_cos = np.cos(twist)[:, None, None, :]
    twist_sin = np.sin(twist)[:, None, None, :]
    inner = angles(width, width, width)
    inner_cos, inner_sin = np.cos(inner), np.sin(inner)
    stage_b = np.concatenate(
        [np.concatenate([inner_cos, -inner_sin], axis=1), np.concatenate([inner_sin, inner_cos], axis=1)],
        axis=0,
    )
    back_b = np.concatenate(
        [np.concatenate([inner_cos, inner_sin], axis=1), np.concatenate([-inner_sin, inner_cos], axis=1)],
        axis=0,
    )
    back_a = np.concatenate([np.cos(outer).T, -np.sin(outer).T], axis=1) / total
    as_f32 = lambda a: jnp.asarray(a.astype(np.float32))
    return tuple(as_f32(a) for a in (stage_a, twist_cos, twist_sin, stage_b, back_b, back_a))


def spectra(stacked, tables):
    stage_a, twist_cos, twist_sin, stage_b, _, _ = tables
    freq_blocks = 2 * stacked.shape[0]
    width = stacked.shape[-1]
    outer = jnp.einsum("kp,pscm->kscm", stage_a, stacked, precision=PRECISE)
    outer_re, outer_im = outer[:freq_blocks], outer[freq_blocks:]
    turned_re = outer_re * twist_cos + outer_im * twist_sin
    turned_im = outer_im * twist_cos - outer_re * twist_sin
    spec = jnp.einsum("kscm,mn->kscn", turned_re, stage_b[:width], precision=PRECISE) + jnp.einsum(
        "kscm,mn->kscn", turned_im, stage_b[width:], precision=PRECISE
    )
    return spec[..., :width], spec[..., width:]


def signals_back(prod_re, prod_im, tables):
    _, twist_cos, twist_sin, _, back_b, back_a = tables
    width = prod_re.shape[-1]
    inner = jnp.einsum("kscn,nm->kscm", prod_re, back_b[:width], precision=PRECISE) + jnp.einsum(
        "kscn,nm->kscm", prod_im, back_b[width:], precision=PRECISE
    )
    inner_re, inner_im = inner[..., :width], inner[..., width:]
    back_re = inner_re * twist_cos - inner_im * twist_sin
    back_im = inner_re * twist_sin + inner_im * twist_cos
    both = jnp.concatenate([back_re, back_im], axis=0)
    return jnp.einsum("pk,kscm->pscm", back_a, both, precision=PRECISE)


def shift_back(x, by, lane):
    earlier = jnp.concatenate([jnp.zeros_like(x[:1]), x[:-1]], axis=0)
    return jnp.where(lane < by, jnp.roll(earlier, by, axis=-1), jnp.roll(x, by, axis=-1))


def shift_ahead(x, by, lane):
    later = jnp.concatenate([x[1:], jnp.zeros_like(x[:1])], axis=0)
    width = x.shape[-1]
    return jnp.where(lane >= width - by, jnp.roll(later, -by, axis=-1), jnp.roll(x, -by, axis=-1))


def to_tokens_in_lanes(block, parts):
    rows, cols = block.shape[-2:]
    swapped = jnp.swapaxes(block, -1, -2)
    return swapped.reshape(block.shape[:-2] + (parts, cols // parts, rows))


def from_tokens_in_lanes(block):
    lead = block.shape[:-3]
    parts, sub, rows = block.shape[-3:]
    return jnp.swapaxes(block.reshape(lead + (parts * sub, rows)), -1, -2)


def split_words(x):
    rounded = lax.reduce_precision(x, exponent_bits=8, mantissa_bits=7)
    return rounded.astype(BF16), (x - rounded).astype(BF16)


def join_words(high, low):
    return high.astype(F32) + low.astype(F32)


def on_device(layer_input, value_pre, gate_act, key_act, short_taps, long_filter, grad_out):
    n_seq = lax.axis_size("seq")
    n_chan = lax.axis_size("chan")
    me = lax.axis_index("seq")
    tap_count = short_taps.shape[0]
    sub = value_pre.shape[1] // n_seq

    half_cols = layer_input.shape[1] // 2
    width = value_pre.shape[0]
    inputs_sc = lax.all_gather(layer_input[:, :half_cols], "seq", axis=0, tiled=True)
    input_slabs = layer_input[:, half_cols:].reshape(width, half_cols // width, width)
    input_slabs = jnp.swapaxes(input_slabs, 0, 1).reshape(-1, sub, width)
    input_slabs = jnp.broadcast_to(input_slabs[:, None], (input_slabs.shape[0], n_seq, sub, width))

    filt_high, filt_low = split_words(long_filter)
    sent = to_tokens_in_lanes(jnp.stack([value_pre, gate_act, key_act, grad_out, filt_high, filt_low]), n_seq)
    sent = jnp.concatenate([sent, input_slabs], axis=0)
    got = lax.all_to_all(sent, "seq", split_axis=1, concat_axis=1, tiled=True)
    chunks = half_cols // width
    inputs_a2a = got[6:].reshape(chunks, width // sub, n_seq, sub, width)
    inputs_a2a = jnp.transpose(inputs_a2a, (2, 1, 3, 0, 4)).reshape(n_seq * width, half_cols)
    value_t = got[0].astype(F32)
    gate_t = got[1].astype(F32)
    key_t = got[2].astype(F32)
    gout_t = got[3].astype(F32)
    filt = join_words(got[4], got[5])
    taps = lax.dynamic_slice_in_dim(short_taps, me * sub, sub, axis=1)[:, :, None]
    lane = lax.broadcasted_iota(jnp.int32, value_t.shape, 2)

    value_shifted = [value_t] + [shift_back(value_t, j, lane) for j in range(1, tap_count)]
    conv_val = taps[0] * value_shifted[0]
    for tap_index in range(1, tap_count):
        conv_val = conv_val + taps[tap_index] * value_shifted[tap_index]
    signal = key_t * conv_val
    grad_mix = gout_t * gate_t
    tables = dft_tables(value_t.shape[0], value_t.shape[2])
    fg_re, fg_im = spectra(jnp.stack([filt, grad_mix], axis=1), tables)
    filt_re, grad_re = fg_re[:, 0:1], fg_re[:, 1:2]
    filt_im, grad_im = fg_im[:, 0:1], fg_im[:, 1:2]
    grad_signal = signals_back(
        filt_re * grad_re + filt_im * grad_im, filt_re * grad_im - filt_im * grad_re, tables
    )[:, 0]
    grad_key = (grad_signal * conv_val).astype(BF16)
    grad_conv = grad_signal * key_t
    value_sum = taps[0] * grad_conv
    for tap_index in range(1, tap_count):
        value_sum = value_sum + taps[tap_index] * shift_ahead(grad_conv, tap_index, lane)
    grad_value = value_sum.astype(BF16)

    swap = [(a * n_chan + b, b * n_chan + a) for a in range(n_seq) for b in range(n_chan)]
    value_swapped = lax.ppermute(grad_value, ("seq", "chan"), swap)
    value_cols = lax.all_gather(value_swapped, "chan", axis=0, tiled=False)

    sig_re, sig_im = spectra(signal[:, None], tables)
    prod_re = jnp.concatenate(
        [filt_re * sig_re - filt_im * sig_im, sig_re * grad_re + sig_im * grad_im], axis=1
    )
    prod_im = jnp.concatenate(
        [filt_re * sig_im + filt_im * sig_re, sig_re * grad_im - sig_im * grad_re], axis=1
    )
    mixed = signals_back(prod_re, prod_im, tables)
    mix_out, grad_filter = mixed[:, 0], mixed[:, 1]
    grad_gate = (gout_t * mix_out).astype(BF16)

    tap_rows = jnp.stack([jnp.sum(grad_conv * value_shifted[j], axis=(0, 2)) for j in range(tap_count)])
    taps_high, taps_low = split_words(tap_rows)
    taps_slab = jnp.pad(jnp.concatenate([taps_high, taps_low], axis=0).T, ((0, 0), (0, width - 2 * tap_count)))
    taps_slab = jnp.broadcast_to(taps_slab[None], value_t.shape)
    gf_high, gf_low = split_words(grad_filter)
    outs = jnp.stack([grad_gate, grad_key, grad_value, gf_high, gf_low, taps_slab])
    outs = lax.all_to_all(outs, "seq", split_axis=1, concat_axis=1, tiled=True)
    taps_got = outs[5, :, :, : 2 * tap_count]
    grad_taps = join_words(taps_got[..., :tap_count], taps_got[..., tap_count:])
    grad_taps = jnp.transpose(grad_taps, (2, 0, 1)).reshape(tap_count, -1)
    outs = from_tokens_in_lanes(outs[:5])
    grad_filter = join_words(outs[3], outs[4])

    blocks = value_t.shape[0]
    parts = []
    for inputs_half in (inputs_sc, inputs_a2a):
        inputs_3 = inputs_half.reshape(blocks, width, inputs_half.shape[1])
        parts.append(jnp.einsum("pmi,cpom->ico", inputs_3, value_cols, preferred_element_type=F32))
    grad_proj = jnp.concatenate(parts, axis=0)
    grad_proj = grad_proj.reshape(grad_proj.shape[0], -1)
    return (outs[0], outs[1], outs[2], grad_taps, grad_filter, grad_proj)


def solution(mesh):
    assert mesh.shape["seq"] == mesh.shape["chan"]
    in_specs = (
        P("seq", "chan"),
        P("seq", "chan"),
        P("seq", "chan"),
        P("seq", "chan"),
        P(None, "chan"),
        P("seq", "chan"),
        P("seq", "chan"),
    )
    out_specs = (
        P("seq", "chan"),
        P("seq", "chan"),
        P("seq", "chan"),
        P(None, "chan"),
        P("seq", "chan"),
        P("chan", "seq"),
    )
    return jax.shard_map(on_device, mesh=mesh, in_specs=in_specs, out_specs=out_specs, check_vma=False)
```

```python
import numpy as np

import jax
import jax.numpy as jnp
from jax import lax
from jax.sharding import PartitionSpec as P


F32 = jnp.float32
BF16 = jnp.bfloat16
PRECISE = lax.Precision.HIGHEST
SEQ = ("y", "x")
CHAN = ("z", "core")


def angles(rows, cols, period):
    product = np.outer(np.arange(rows), np.arange(cols)) % period
    return product.astype(np.float64) * (2.0 * np.pi / period)


def dft_tables(blocks, width):
    freq_blocks = 2 * blocks
    total = freq_blocks * width
    outer = angles(freq_blocks, blocks, freq_blocks)
    stage_a = np.concatenate([np.cos(outer), -np.sin(outer)], axis=0)
    twist = angles(freq_blocks, width, total)
    twist_cos = np.cos(twist)[:, None, None, :]
    twist_sin = np.sin(twist)[:, None, None, :]
    inner = angles(width, width, width)
    inner_cos, inner_sin = np.cos(inner), np.sin(inner)
    stage_b = np.concatenate(
        [np.concatenate([inner_cos, -inner_sin], axis=1), np.concatenate([inner_sin, inner_cos], axis=1)],
        axis=0,
    )
    back_b = np.concatenate(
        [np.concatenate([inner_cos, inner_sin], axis=1), np.concatenate([-inner_sin, inner_cos], axis=1)],
        axis=0,
    )
    back_a = np.concatenate([np.cos(outer).T, -np.sin(outer).T], axis=1) / total
    as_f32 = lambda a: jnp.asarray(a.astype(np.float32))
    return tuple(as_f32(a) for a in (stage_a, twist_cos, twist_sin, stage_b, back_b, back_a))


def spectra(stacked, tables):
    stage_a, twist_cos, twist_sin, stage_b, _, _ = tables
    freq_blocks = 2 * stacked.shape[0]
    width = stacked.shape[-1]
    outer = jnp.einsum("kp,pscm->kscm", stage_a, stacked, precision=PRECISE)
    outer_re, outer_im = outer[:freq_blocks], outer[freq_blocks:]
    turned_re = outer_re * twist_cos + outer_im * twist_sin
    turned_im = outer_im * twist_cos - outer_re * twist_sin
    spec = jnp.einsum("kscm,mn->kscn", turned_re, stage_b[:width], precision=PRECISE) + jnp.einsum(
        "kscm,mn->kscn", turned_im, stage_b[width:], precision=PRECISE
    )
    return spec[..., :width], spec[..., width:]


def signals_back(prod_re, prod_im, tables):
    _, twist_cos, twist_sin, _, back_b, back_a = tables
    width = prod_re.shape[-1]
    inner = jnp.einsum("kscn,nm->kscm", prod_re, back_b[:width], precision=PRECISE) + jnp.einsum(
        "kscn,nm->kscm", prod_im, back_b[width:], precision=PRECISE
    )
    inner_re, inner_im = inner[..., :width], inner[..., width:]
    back_re = inner_re * twist_cos - inner_im * twist_sin
    back_im = inner_re * twist_sin + inner_im * twist_cos
    both = jnp.concatenate([back_re, back_im], axis=0)
    return jnp.einsum("pk,kscm->pscm", back_a, both, precision=PRECISE)


def shift_back(x, by, lane):
    earlier = jnp.concatenate([jnp.zeros_like(x[:1]), x[:-1]], axis=0)
    return jnp.where(lane < by, jnp.roll(earlier, by, axis=-1), jnp.roll(x, by, axis=-1))


def shift_ahead(x, by, lane):
    later = jnp.concatenate([x[1:], jnp.zeros_like(x[:1])], axis=0)
    width = x.shape[-1]
    return jnp.where(lane >= width - by, jnp.roll(later, -by, axis=-1), jnp.roll(x, -by, axis=-1))


def to_tokens_in_lanes(block, parts):
    rows, cols = block.shape[-2:]
    swapped = jnp.swapaxes(block, -1, -2)
    return swapped.reshape(block.shape[:-2] + (parts, cols // parts, rows))


def from_tokens_in_lanes(block):
    lead = block.shape[:-3]
    parts, sub, rows = block.shape[-3:]
    return jnp.swapaxes(block.reshape(lead + (parts * sub, rows)), -1, -2)


def split_words(x):
    rounded = lax.reduce_precision(x, exponent_bits=8, mantissa_bits=7)
    return rounded.astype(BF16), (x - rounded).astype(BF16)


def join_words(high, low):
    return high.astype(F32) + low.astype(F32)


def on_device(layer_input, value_pre, gate_act, key_act, short_taps, long_filter, grad_out):
    n_seq = lax.axis_size(SEQ)
    n_chan = lax.axis_size(CHAN)
    me = lax.axis_index(SEQ)
    tap_count = short_taps.shape[0]
    sub = value_pre.shape[1] // n_seq

    inputs_all = lax.all_gather(layer_input, "x", axis=0, tiled=True)
    inputs_all = lax.all_gather(inputs_all, "y", axis=0, tiled=True)

    filt_high, filt_low = split_words(long_filter)
    sent = to_tokens_in_lanes(jnp.stack([value_pre, gate_act, key_act, grad_out, filt_high, filt_low]), n_seq)
    got = lax.all_to_all(sent, SEQ, split_axis=1, concat_axis=1, tiled=True)
    value_t = got[0].astype(F32)
    gate_t = got[1].astype(F32)
    key_t = got[2].astype(F32)
    gout_t = got[3].astype(F32)
    filt = join_words(got[4], got[5])
    taps = lax.dynamic_slice_in_dim(short_taps, me * sub, sub, axis=1)[:, :, None]
    lane = lax.broadcasted_iota(jnp.int32, value_t.shape, 2)

    value_shifted = [value_t] + [shift_back(value_t, j, lane) for j in range(1, tap_count)]
    conv_val = taps[0] * value_shifted[0]
    for tap_index in range(1, tap_count):
        conv_val = conv_val + taps[tap_index] * value_shifted[tap_index]
    signal = key_t * conv_val
    grad_mix = gout_t * gate_t
    tables = dft_tables(value_t.shape[0], value_t.shape[2])
    fg_re, fg_im = spectra(jnp.stack([filt, grad_mix], axis=1), tables)
    filt_re, grad_re = fg_re[:, 0:1], fg_re[:, 1:2]
    filt_im, grad_im = fg_im[:, 0:1], fg_im[:, 1:2]
    grad_signal = signals_back(
        filt_re * grad_re + filt_im * grad_im, filt_re * grad_im - filt_im * grad_re, tables
    )[:, 0]
    grad_key = (grad_signal * conv_val).astype(BF16)
    grad_conv = grad_signal * key_t
    value_sum = taps[0] * grad_conv
    for tap_index in range(1, tap_count):
        value_sum = value_sum + taps[tap_index] * shift_ahead(grad_conv, tap_index, lane)
    grad_value = value_sum.astype(BF16)

    swap = [(a * n_chan + b, b * n_chan + a) for a in range(n_seq) for b in range(n_chan)]
    value_swapped = lax.ppermute(grad_value, SEQ + CHAN, swap)
    value_cols = lax.all_gather(value_swapped, "core", axis=0, tiled=False)
    value_cols = lax.all_gather(value_cols, "z", axis=0, tiled=False)
    value_cols = value_cols.reshape((-1,) + value_swapped.shape)

    sig_re, sig_im = spectra(signal[:, None], tables)
    prod_re = jnp.concatenate(
        [filt_re * sig_re - filt_im * sig_im, sig_re * grad_re + sig_im * grad_im], axis=1
    )
    prod_im = jnp.concatenate(
        [filt_re * sig_im + filt_im * sig_re, sig_re * grad_im - sig_im * grad_re], axis=1
    )
    mixed = signals_back(prod_re, prod_im, tables)
    mix_out, grad_filter = mixed[:, 0], mixed[:, 1]
    grad_gate = (gout_t * mix_out).astype(BF16)

    tap_rows = jnp.stack([jnp.sum(grad_conv * value_shifted[j], axis=(0, 2)) for j in range(tap_count)])
    taps_high, taps_low = split_words(tap_rows)
    width = value_t.shape[2]
    taps_slab = jnp.pad(jnp.concatenate([taps_high, taps_low], axis=0).T, ((0, 0), (0, width - 2 * tap_count)))
    taps_slab = jnp.broadcast_to(taps_slab[None], value_t.shape)
    gf_high, gf_low = split_words(grad_filter)
    outs = jnp.stack([grad_gate, grad_key, grad_value, gf_high, gf_low, taps_slab])
    outs = lax.all_to_all(outs, SEQ, split_axis=1, concat_axis=1, tiled=True)
    taps_got = outs[5, :, :, : 2 * tap_count]
    grad_taps = join_words(taps_got[..., :tap_count], taps_got[..., tap_count:])
    grad_taps = jnp.transpose(grad_taps, (2, 0, 1)).reshape(tap_count, -1)
    outs = from_tokens_in_lanes(outs[:5])
    grad_filter = join_words(outs[3], outs[4])

    blocks = value_t.shape[0]
    inputs_3 = inputs_all.reshape(blocks, width, inputs_all.shape[1])
    grad_proj = jnp.einsum("pmi,cpom->ico", inputs_3, value_cols, preferred_element_type=F32)
    grad_proj = grad_proj.reshape(grad_proj.shape[0], -1)
    return (outs[0], outs[1], outs[2], grad_taps, grad_filter, grad_proj)


def solution(mesh):
    seq_size, chan_size = mesh.shape["seq"], mesh.shape["chan"]
    assert seq_size == chan_size and seq_size % 4 == 0 and chan_size % 2 == 0
    grid = mesh.devices.reshape(4, seq_size // 4, chan_size // 2, 2)
    fine = jax.sharding.Mesh(grid, ("y", "x", "z", "core"))
    rows = P(SEQ, CHAN)
    in_specs = (rows, rows, rows, rows, P(None, CHAN), rows, rows)
    out_specs = (rows, rows, rows, P(None, CHAN), rows, P(CHAN, SEQ))
    return jax.shard_map(on_device, mesh=fine, in_specs=in_specs, out_specs=out_specs, check_vma=False)
```

```python
import numpy as np

import jax
import jax.numpy as jnp
from jax import lax
from jax.sharding import PartitionSpec as P


F32 = jnp.float32
BF16 = jnp.bfloat16
PRECISE = lax.Precision.HIGHEST


def angles(rows, cols, period):
    product = np.outer(np.arange(rows), np.arange(cols)) % period
    return product.astype(np.float64) * (2.0 * np.pi / period)


def dft_tables(blocks, width):
    freq_blocks = 2 * blocks
    total = freq_blocks * width
    outer = angles(freq_blocks, blocks, freq_blocks)
    stage_a = np.concatenate([np.cos(outer), -np.sin(outer)], axis=0)
    twist = angles(freq_blocks, width, total)
    twist_cos = np.cos(twist)[:, None, None, :]
    twist_sin = np.sin(twist)[:, None, None, :]
    inner = angles(width, width, width)
    inner_cos, inner_sin = np.cos(inner), np.sin(inner)
    stage_b = np.concatenate(
        [np.concatenate([inner_cos, -inner_sin], axis=1), np.concatenate([inner_sin, inner_cos], axis=1)],
        axis=0,
    )
    back_b = np.concatenate(
        [np.concatenate([inner_cos, inner_sin], axis=1), np.concatenate([-inner_sin, inner_cos], axis=1)],
        axis=0,
    )
    back_a = np.concatenate([np.cos(outer).T, -np.sin(outer).T], axis=1) / total
    as_f32 = lambda a: jnp.asarray(a.astype(np.float32))
    return tuple(as_f32(a) for a in (stage_a, twist_cos, twist_sin, stage_b, back_b, back_a))


def spectra(stacked, tables):
    stage_a, twist_cos, twist_sin, stage_b, _, _ = tables
    freq_blocks = 2 * stacked.shape[0]
    width = stacked.shape[-1]
    outer = jnp.einsum("kp,pscm->kscm", stage_a, stacked, precision=PRECISE)
    outer_re, outer_im = outer[:freq_blocks], outer[freq_blocks:]
    turned_re = outer_re * twist_cos + outer_im * twist_sin
    turned_im = outer_im * twist_cos - outer_re * twist_sin
    spec = jnp.einsum("kscm,mn->kscn", turned_re, stage_b[:width], precision=PRECISE) + jnp.einsum(
        "kscm,mn->kscn", turned_im, stage_b[width:], precision=PRECISE
    )
    return spec[..., :width], spec[..., width:]


def signals_back(prod_re, prod_im, tables):
    _, twist_cos, twist_sin, _, back_b, back_a = tables
    width = prod_re.shape[-1]
    inner = jnp.einsum("kscn,nm->kscm", prod_re, back_b[:width], precision=PRECISE) + jnp.einsum(
        "kscn,nm->kscm", prod_im, back_b[width:], precision=PRECISE
    )
    inner_re, inner_im = inner[..., :width], inner[..., width:]
    back_re = inner_re * twist_cos - inner_im * twist_sin
    back_im = inner_re * twist_sin + inner_im * twist_cos
    both = jnp.concatenate([back_re, back_im], axis=0)
    return jnp.einsum("pk,kscm->pscm", back_a, both, precision=PRECISE)


def shift_back(x, by, lane):
    earlier = jnp.concatenate([jnp.zeros_like(x[:1]), x[:-1]], axis=0)
    return jnp.where(lane < by, jnp.roll(earlier, by, axis=-1), jnp.roll(x, by, axis=-1))


def shift_ahead(x, by, lane):
    later = jnp.concatenate([x[1:], jnp.zeros_like(x[:1])], axis=0)
    width = x.shape[-1]
    return jnp.where(lane >= width - by, jnp.roll(later, -by, axis=-1), jnp.roll(x, -by, axis=-1))


def to_tokens_in_lanes(block, parts):
    rows, cols = block.shape[-2:]
    swapped = jnp.swapaxes(block, -1, -2)
    return swapped.reshape(block.shape[:-2] + (parts, cols // parts, rows))


def from_tokens_in_lanes(block):
    lead = block.shape[:-3]
    parts, sub, rows = block.shape[-3:]
    return jnp.swapaxes(block.reshape(lead + (parts * sub, rows)), -1, -2)


def split_words(x):
    rounded = lax.reduce_precision(x, exponent_bits=8, mantissa_bits=7)
    return rounded.astype(BF16), (x - rounded).astype(BF16)


def join_words(high, low):
    return high.astype(F32) + low.astype(F32)


def on_device(layer_input, value_pre, gate_act, key_act, short_taps, long_filter, grad_out):
    n_seq = lax.axis_size("seq")
    n_chan = lax.axis_size("chan")
    me = lax.axis_index("seq")
    tap_count = short_taps.shape[0]
    sub = value_pre.shape[1] // n_seq

    inputs_all = lax.all_gather(layer_input, "seq", axis=0, tiled=True)

    filt_high, filt_low = split_words(long_filter)
    sent = to_tokens_in_lanes(jnp.stack([value_pre, gate_act, key_act, grad_out, filt_high, filt_low]), n_seq)
    got = lax.all_to_all(sent, "seq", split_axis=1, concat_axis=1, tiled=True)
    value_t = got[0].astype(F32)
    gate_t = got[1].astype(F32)
    key_t = got[2].astype(F32)
    gout_t = got[3].astype(F32)
    filt = join_words(got[4], got[5])
    taps = lax.dynamic_slice_in_dim(short_taps, me * sub, sub, axis=1)[:, :, None]
    lane = lax.broadcasted_iota(jnp.int32, value_t.shape, 2)

    value_shifted = [value_t] + [shift_back(value_t, j, lane) for j in range(1, tap_count)]
    conv_val = taps[0] * value_shifted[0]
    for tap_index in range(1, tap_count):
        conv_val = conv_val + taps[tap_index] * value_shifted[tap_index]
    signal = key_t * conv_val
    grad_mix = gout_t * gate_t
    tables = dft_tables(value_t.shape[0], value_t.shape[2])
    fg_re, fg_im = spectra(jnp.stack([filt, grad_mix], axis=1), tables)
    filt_re, grad_re = fg_re[:, 0:1], fg_re[:, 1:2]
    filt_im, grad_im = fg_im[:, 0:1], fg_im[:, 1:2]
    grad_signal = signals_back(
        filt_re * grad_re + filt_im * grad_im, filt_re * grad_im - filt_im * grad_re, tables
    )[:, 0]
    grad_key = (grad_signal * conv_val).astype(BF16)
    grad_conv = grad_signal * key_t
    value_sum = taps[0] * grad_conv
    for tap_index in range(1, tap_count):
        value_sum = value_sum + taps[tap_index] * shift_ahead(grad_conv, tap_index, lane)
    grad_value = value_sum.astype(BF16)

    grad_value, signal, filt_re, filt_im, grad_re, grad_im = lax.optimization_barrier(
        (grad_value, signal, filt_re, filt_im, grad_re, grad_im)
    )
    swap = [(a * n_chan + b, b * n_chan + a) for a in range(n_seq) for b in range(n_chan)]
    value_swapped = lax.ppermute(grad_value, ("seq", "chan"), swap)
    value_cols = lax.all_gather(value_swapped, "chan", axis=0, tiled=False)

    sig_re, sig_im = spectra(signal[:, None], tables)
    prod_re = jnp.concatenate(
        [filt_re * sig_re - filt_im * sig_im, sig_re * grad_re + sig_im * grad_im], axis=1
    )
    prod_im = jnp.concatenate(
        [filt_re * sig_im + filt_im * sig_re, sig_re * grad_im - sig_im * grad_re], axis=1
    )
    mixed = signals_back(prod_re, prod_im, tables)
    mix_out, grad_filter = mixed[:, 0], mixed[:, 1]
    grad_gate = (gout_t * mix_out).astype(BF16)

    tap_rows = jnp.stack([jnp.sum(grad_conv * value_shifted[j], axis=(0, 2)) for j in range(tap_count)])
    taps_high, taps_low = split_words(tap_rows)
    width = value_t.shape[2]
    taps_slab = jnp.pad(jnp.concatenate([taps_high, taps_low], axis=0).T, ((0, 0), (0, width - 2 * tap_count)))
    taps_slab = jnp.broadcast_to(taps_slab[None], value_t.shape)
    gf_high, gf_low = split_words(grad_filter)
    outs = jnp.stack([grad_gate, grad_key, grad_value, gf_high, gf_low, taps_slab])
    outs = lax.all_to_all(outs, "seq", split_axis=1, concat_axis=1, tiled=True)
    taps_got = outs[5, :, :, : 2 * tap_count]
    grad_taps = join_words(taps_got[..., :tap_count], taps_got[..., tap_count:])
    grad_taps = jnp.transpose(grad_taps, (2, 0, 1)).reshape(tap_count, -1)
    outs = from_tokens_in_lanes(outs[:5])
    grad_filter = join_words(outs[3], outs[4])

    blocks = value_t.shape[0]
    inputs_3 = inputs_all.reshape(blocks, width, inputs_all.shape[1])
    grad_proj = jnp.einsum("pmi,cpom->ico", inputs_3, value_cols, preferred_element_type=F32)
    grad_proj = grad_proj.reshape(grad_proj.shape[0], -1)
    return (outs[0], outs[1], outs[2], grad_taps, grad_filter, grad_proj)


def solution(mesh):
    assert mesh.shape["seq"] == mesh.shape["chan"]
    in_specs = (
        P("seq", "chan"),
        P("seq", "chan"),
        P("seq", "chan"),
        P("seq", "chan"),
        P(None, "chan"),
        P("seq", "chan"),
        P("seq", "chan"),
    )
    out_specs = (
        P("seq", "chan"),
        P("seq", "chan"),
        P("seq", "chan"),
        P(None, "chan"),
        P("seq", "chan"),
        P("chan", "seq"),
    )
    return jax.shard_map(on_device, mesh=mesh, in_specs=in_specs, out_specs=out_specs, check_vma=False)
```

```python
import numpy as np

import jax
import jax.numpy as jnp
from jax import lax
from jax.sharding import PartitionSpec as P


F32 = jnp.float32
BF16 = jnp.bfloat16
PRECISE = lax.Precision.HIGHEST


def angles(rows, cols, period):
    product = np.outer(np.arange(rows), np.arange(cols)) % period
    return product.astype(np.float64) * (2.0 * np.pi / period)


def dft_tables(blocks, width):
    freq_blocks = 2 * blocks
    total = freq_blocks * width
    outer = angles(freq_blocks, blocks, freq_blocks)
    stage_a = np.concatenate([np.cos(outer), -np.sin(outer)], axis=0)
    twist = angles(freq_blocks, width, total)
    twist_cos = np.cos(twist)[:, None, None, :]
    twist_sin = np.sin(twist)[:, None, None, :]
    back_a = np.concatenate([np.cos(outer).T, -np.sin(outer).T], axis=1) / total
    as_f32 = lambda a: jnp.asarray(a.astype(np.float32))
    rows = lax.broadcasted_iota(jnp.int32, (width, width), 0)
    cols = lax.broadcasted_iota(jnp.int32, (width, width), 1)
    product = lax.optimization_barrier(rows * cols % width)
    inner = product.astype(F32) * (2.0 * np.pi / width)
    inner_cos, inner_sin = jnp.cos(inner), jnp.sin(inner)
    stage_b = jnp.concatenate(
        [jnp.concatenate([inner_cos, -inner_sin], axis=1), jnp.concatenate([inner_sin, inner_cos], axis=1)],
        axis=0,
    )
    back_b = jnp.concatenate(
        [jnp.concatenate([inner_cos, inner_sin], axis=1), jnp.concatenate([-inner_sin, inner_cos], axis=1)],
        axis=0,
    )
    stage_a, twist_cos, twist_sin, back_a = (as_f32(a) for a in (stage_a, twist_cos, twist_sin, back_a))
    return stage_a, twist_cos, twist_sin, stage_b, back_b, back_a


def spectra(stacked, tables):
    stage_a, twist_cos, twist_sin, stage_b, _, _ = tables
    freq_blocks = 2 * stacked.shape[0]
    width = stacked.shape[-1]
    outer = jnp.einsum("kp,pscm->kscm", stage_a, stacked, precision=PRECISE)
    outer_re, outer_im = outer[:freq_blocks], outer[freq_blocks:]
    turned_re = outer_re * twist_cos + outer_im * twist_sin
    turned_im = outer_im * twist_cos - outer_re * twist_sin
    spec = jnp.einsum("kscm,mn->kscn", turned_re, stage_b[:width], precision=PRECISE) + jnp.einsum(
        "kscm,mn->kscn", turned_im, stage_b[width:], precision=PRECISE
    )
    return spec[..., :width], spec[..., width:]


def signals_back(prod_re, prod_im, tables):
    _, twist_cos, twist_sin, _, back_b, back_a = tables
    width = prod_re.shape[-1]
    inner = jnp.einsum("kscn,nm->kscm", prod_re, back_b[:width], precision=PRECISE) + jnp.einsum(
        "kscn,nm->kscm", prod_im, back_b[width:], precision=PRECISE
    )
    inner_re, inner_im = inner[..., :width], inner[..., width:]
    back_re = inner_re * twist_cos - inner_im * twist_sin
    back_im = inner_re * twist_sin + inner_im * twist_cos
    both = jnp.concatenate([back_re, back_im], axis=0)
    return jnp.einsum("pk,kscm->pscm", back_a, both, precision=PRECISE)


def shift_back(x, by, lane):
    earlier = jnp.concatenate([jnp.zeros_like(x[:1]), x[:-1]], axis=0)
    return jnp.where(lane < by, jnp.roll(earlier, by, axis=-1), jnp.roll(x, by, axis=-1))


def shift_ahead(x, by, lane):
    later = jnp.concatenate([x[1:], jnp.zeros_like(x[:1])], axis=0)
    width = x.shape[-1]
    return jnp.where(lane >= width - by, jnp.roll(later, -by, axis=-1), jnp.roll(x, -by, axis=-1))


def to_tokens_in_lanes(block, parts):
    rows, cols = block.shape[-2:]
    swapped = jnp.swapaxes(block, -1, -2)
    return swapped.reshape(block.shape[:-2] + (parts, cols // parts, rows))


def from_tokens_in_lanes(block):
    lead = block.shape[:-3]
    parts, sub, rows = block.shape[-3:]
    return jnp.swapaxes(block.reshape(lead + (parts * sub, rows)), -1, -2)


def split_words(x):
    rounded = lax.reduce_precision(x, exponent_bits=8, mantissa_bits=7)
    return rounded.astype(BF16), (x - rounded).astype(BF16)


def join_words(high, low):
    return high.astype(F32) + low.astype(F32)


def on_device(layer_input, value_pre, gate_act, key_act, short_taps, long_filter, grad_out):
    n_seq = lax.axis_size("seq")
    n_chan = lax.axis_size("chan")
    me = lax.axis_index("seq")
    tap_count = short_taps.shape[0]
    sub = value_pre.shape[1] // n_seq

    inputs_all = lax.all_gather(layer_input, "seq", axis=0, tiled=True)

    filt_high, filt_low = split_words(long_filter)
    sent = to_tokens_in_lanes(jnp.stack([value_pre, gate_act, key_act, grad_out, filt_high, filt_low]), n_seq)
    got = lax.all_to_all(sent, "seq", split_axis=1, concat_axis=1, tiled=True)
    value_t = got[0].astype(F32)
    gate_t = got[1].astype(F32)
    key_t = got[2].astype(F32)
    gout_t = got[3].astype(F32)
    filt = join_words(got[4], got[5])
    taps = lax.dynamic_slice_in_dim(short_taps, me * sub, sub, axis=1)[:, :, None]
    lane = lax.broadcasted_iota(jnp.int32, value_t.shape, 2)

    value_shifted = [value_t] + [shift_back(value_t, j, lane) for j in range(1, tap_count)]
    conv_val = taps[0] * value_shifted[0]
    for tap_index in range(1, tap_count):
        conv_val = conv_val + taps[tap_index] * value_shifted[tap_index]
    signal = key_t * conv_val
    grad_mix = gout_t * gate_t
    tables = dft_tables(value_t.shape[0], value_t.shape[2])
    fg_re, fg_im = spectra(jnp.stack([filt, grad_mix], axis=1), tables)
    filt_re, grad_re = fg_re[:, 0:1], fg_re[:, 1:2]
    filt_im, grad_im = fg_im[:, 0:1], fg_im[:, 1:2]
    grad_signal = signals_back(
        filt_re * grad_re + filt_im * grad_im, filt_re * grad_im - filt_im * grad_re, tables
    )[:, 0]
    grad_key = (grad_signal * conv_val).astype(BF16)
    grad_conv = grad_signal * key_t
    value_sum = taps[0] * grad_conv
    for tap_index in range(1, tap_count):
        value_sum = value_sum + taps[tap_index] * shift_ahead(grad_conv, tap_index, lane)
    grad_value = value_sum.astype(BF16)

    grad_value, signal, filt_re, filt_im, grad_re, grad_im = lax.optimization_barrier(
        (grad_value, signal, filt_re, filt_im, grad_re, grad_im)
    )
    swap = [(a * n_chan + b, b * n_chan + a) for a in range(n_seq) for b in range(n_chan)]
    value_swapped = lax.ppermute(grad_value, ("seq", "chan"), swap)
    value_cols = lax.all_gather(value_swapped, "chan", axis=0, tiled=False)

    sig_re, sig_im = spectra(signal[:, None], tables)
    prod_re = jnp.concatenate(
        [filt_re * sig_re - filt_im * sig_im, sig_re * grad_re + sig_im * grad_im], axis=1
    )
    prod_im = jnp.concatenate(
        [filt_re * sig_im + filt_im * sig_re, sig_re * grad_im - sig_im * grad_re], axis=1
    )
    mixed = signals_back(prod_re, prod_im, tables)
    mix_out, grad_filter = mixed[:, 0], mixed[:, 1]
    grad_gate = (gout_t * mix_out).astype(BF16)

    tap_rows = jnp.stack([jnp.sum(grad_conv * value_shifted[j], axis=(0, 2)) for j in range(tap_count)])
    taps_high, taps_low = split_words(tap_rows)
    width = value_t.shape[2]
    taps_slab = jnp.pad(jnp.concatenate([taps_high, taps_low], axis=0).T, ((0, 0), (0, width - 2 * tap_count)))
    taps_slab = jnp.broadcast_to(taps_slab[None], value_t.shape)
    gf_high, gf_low = split_words(grad_filter)
    outs = jnp.stack([grad_gate, grad_key, grad_value, gf_high, gf_low, taps_slab])
    outs = lax.all_to_all(outs, "seq", split_axis=1, concat_axis=1, tiled=True)
    taps_got = outs[5, :, :, : 2 * tap_count]
    grad_taps = join_words(taps_got[..., :tap_count], taps_got[..., tap_count:])
    grad_taps = jnp.transpose(grad_taps, (2, 0, 1)).reshape(tap_count, -1)
    outs = from_tokens_in_lanes(outs[:5])
    grad_filter = join_words(outs[3], outs[4])

    blocks = value_t.shape[0]
    inputs_3 = inputs_all.reshape(blocks, width, inputs_all.shape[1])
    grad_proj = jnp.einsum("pmi,cpom->ico", inputs_3, value_cols, preferred_element_type=F32)
    grad_proj = grad_proj.reshape(grad_proj.shape[0], -1)
    return (outs[0], outs[1], outs[2], grad_taps, grad_filter, grad_proj)


def solution(mesh):
    assert mesh.shape["seq"] == mesh.shape["chan"]
    in_specs = (
        P("seq", "chan"),
        P("seq", "chan"),
        P("seq", "chan"),
        P("seq", "chan"),
        P(None, "chan"),
        P("seq", "chan"),
        P("seq", "chan"),
    )
    out_specs = (
        P("seq", "chan"),
        P("seq", "chan"),
        P("seq", "chan"),
        P(None, "chan"),
        P("seq", "chan"),
        P("chan", "seq"),
    )
    return jax.shard_map(on_device, mesh=mesh, in_specs=in_specs, out_specs=out_specs, check_vma=False)
```

```python
import numpy as np

import jax
import jax.numpy as jnp
from jax import lax
from jax.sharding import PartitionSpec as P


F32 = jnp.float32
BF16 = jnp.bfloat16
PRECISE = lax.Precision.HIGHEST
SEQ = ("y", "x")
SEQ_NAME, CHAN_NAME = "seq", "chan"
CHAN = ("z", "core")


def angles(rows, cols, period):
    product = np.outer(np.arange(rows), np.arange(cols)) % period
    return product.astype(np.float64) * (2.0 * np.pi / period)


def dft_tables(blocks, width):
    freq_blocks = 2 * blocks
    total = freq_blocks * width
    outer = angles(freq_blocks, blocks, freq_blocks)
    stage_a = np.concatenate([np.cos(outer), -np.sin(outer)], axis=0)
    twist = angles(freq_blocks, width, total)
    twist_cos = np.cos(twist)[:, None, None, :]
    twist_sin = np.sin(twist)[:, None, None, :]
    back_a = np.concatenate([np.cos(outer).T, -np.sin(outer).T], axis=1) / total
    as_f32 = lambda a: jnp.asarray(a.astype(np.float32))
    rows = lax.broadcasted_iota(jnp.int32, (width, width), 0)
    cols = lax.broadcasted_iota(jnp.int32, (width, width), 1)
    product = lax.optimization_barrier(rows * cols % width)
    inner = product.astype(F32) * (2.0 * np.pi / width)
    inner_cos, inner_sin = jnp.cos(inner), jnp.sin(inner)
    stage_b = jnp.concatenate(
        [jnp.concatenate([inner_cos, -inner_sin], axis=1), jnp.concatenate([inner_sin, inner_cos], axis=1)],
        axis=0,
    )
    back_b = jnp.concatenate(
        [jnp.concatenate([inner_cos, inner_sin], axis=1), jnp.concatenate([-inner_sin, inner_cos], axis=1)],
        axis=0,
    )
    stage_a, twist_cos, twist_sin, back_a = (as_f32(a) for a in (stage_a, twist_cos, twist_sin, back_a))
    return stage_a, twist_cos, twist_sin, stage_b, back_b, back_a


def spectra(stacked, tables):
    stage_a, twist_cos, twist_sin, stage_b, _, _ = tables
    freq_blocks = 2 * stacked.shape[0]
    width = stacked.shape[-1]
    outer = jnp.einsum("kp,pscm->kscm", stage_a, stacked, precision=PRECISE)
    outer_re, outer_im = outer[:freq_blocks], outer[freq_blocks:]
    turned_re = outer_re * twist_cos + outer_im * twist_sin
    turned_im = outer_im * twist_cos - outer_re * twist_sin
    spec = jnp.einsum("kscm,mn->kscn", turned_re, stage_b[:width], precision=PRECISE) + jnp.einsum(
        "kscm,mn->kscn", turned_im, stage_b[width:], precision=PRECISE
    )
    return spec[..., :width], spec[..., width:]


def signals_back(prod_re, prod_im, tables):
    _, twist_cos, twist_sin, _, back_b, back_a = tables
    width = prod_re.shape[-1]
    inner = jnp.einsum("kscn,nm->kscm", prod_re, back_b[:width], precision=PRECISE) + jnp.einsum(
        "kscn,nm->kscm", prod_im, back_b[width:], precision=PRECISE
    )
    inner_re, inner_im = inner[..., :width], inner[..., width:]
    back_re = inner_re * twist_cos - inner_im * twist_sin
    back_im = inner_re * twist_sin + inner_im * twist_cos
    both = jnp.concatenate([back_re, back_im], axis=0)
    return jnp.einsum("pk,kscm->pscm", back_a, both, precision=PRECISE)


def shift_back(x, by, lane):
    earlier = jnp.concatenate([jnp.zeros_like(x[:1]), x[:-1]], axis=0)
    return jnp.where(lane < by, jnp.roll(earlier, by, axis=-1), jnp.roll(x, by, axis=-1))


def shift_ahead(x, by, lane):
    later = jnp.concatenate([x[1:], jnp.zeros_like(x[:1])], axis=0)
    width = x.shape[-1]
    return jnp.where(lane >= width - by, jnp.roll(later, -by, axis=-1), jnp.roll(x, -by, axis=-1))


def to_tokens_in_lanes(block, parts):
    rows, cols = block.shape[-2:]
    swapped = jnp.swapaxes(block, -1, -2)
    return swapped.reshape(block.shape[:-2] + (parts, cols // parts, rows))


def from_tokens_in_lanes(block):
    lead = block.shape[:-3]
    parts, sub, rows = block.shape[-3:]
    return jnp.swapaxes(block.reshape(lead + (parts * sub, rows)), -1, -2)


def split_words(x):
    rounded = lax.reduce_precision(x, exponent_bits=8, mantissa_bits=7)
    return rounded.astype(BF16), (x - rounded).astype(BF16)


def join_words(high, low):
    return high.astype(F32) + low.astype(F32)


def on_device(layer_input, value_pre, gate_act, key_act, short_taps, long_filter, grad_out):
    n_seq = lax.axis_size(SEQ)
    n_chan = lax.axis_size(CHAN)
    me = lax.axis_index(SEQ)
    tap_count = short_taps.shape[0]
    sub = value_pre.shape[1] // n_seq

    inputs_all = lax.all_gather(layer_input, "x", axis=0, tiled=True)
    inputs_all = lax.all_gather(inputs_all, "y", axis=0, tiled=True)

    filt_high, filt_low = split_words(long_filter)
    sent = to_tokens_in_lanes(jnp.stack([value_pre, gate_act, key_act, grad_out, filt_high, filt_low]), n_seq)
    got = lax.all_to_all(sent, SEQ, split_axis=1, concat_axis=1, tiled=True)
    value_t = got[0].astype(F32)
    gate_t = got[1].astype(F32)
    key_t = got[2].astype(F32)
    gout_t = got[3].astype(F32)
    filt = join_words(got[4], got[5])
    taps = lax.dynamic_slice_in_dim(short_taps, me * sub, sub, axis=1)[:, :, None]
    lane = lax.broadcasted_iota(jnp.int32, value_t.shape, 2)

    value_shifted = [value_t] + [shift_back(value_t, j, lane) for j in range(1, tap_count)]
    conv_val = taps[0] * value_shifted[0]
    for tap_index in range(1, tap_count):
        conv_val = conv_val + taps[tap_index] * value_shifted[tap_index]
    signal = key_t * conv_val
    grad_mix = gout_t * gate_t
    tables = dft_tables(value_t.shape[0], value_t.shape[2])
    fg_re, fg_im = spectra(jnp.stack([filt, grad_mix], axis=1), tables)
    filt_re, grad_re = fg_re[:, 0:1], fg_re[:, 1:2]
    filt_im, grad_im = fg_im[:, 0:1], fg_im[:, 1:2]
    grad_signal = signals_back(
        filt_re * grad_re + filt_im * grad_im, filt_re * grad_im - filt_im * grad_re, tables
    )[:, 0]
    grad_key = (grad_signal * conv_val).astype(BF16)
    grad_conv = grad_signal * key_t
    value_sum = taps[0] * grad_conv
    for tap_index in range(1, tap_count):
        value_sum = value_sum + taps[tap_index] * shift_ahead(grad_conv, tap_index, lane)
    grad_value = value_sum.astype(BF16)

    grad_value, signal, filt_re, filt_im, grad_re, grad_im = lax.optimization_barrier(
        (grad_value, signal, filt_re, filt_im, grad_re, grad_im)
    )
    swap = [(a * n_chan + b, b * n_chan + a) for a in range(n_seq) for b in range(n_chan)]
    value_swapped = lax.ppermute(grad_value, SEQ + CHAN, swap)
    value_cols = lax.all_gather(value_swapped, CHAN, axis=0, tiled=False)

    sig_re, sig_im = spectra(signal[:, None], tables)
    prod_re = jnp.concatenate(
        [filt_re * sig_re - filt_im * sig_im, sig_re * grad_re + sig_im * grad_im], axis=1
    )
    prod_im = jnp.concatenate(
        [filt_re * sig_im + filt_im * sig_re, sig_re * grad_im - sig_im * grad_re], axis=1
    )
    mixed = signals_back(prod_re, prod_im, tables)
    mix_out, grad_filter = mixed[:, 0], mixed[:, 1]
    grad_gate = (gout_t * mix_out).astype(BF16)

    tap_rows = jnp.stack([jnp.sum(grad_conv * value_shifted[j], axis=(0, 2)) for j in range(tap_count)])
    taps_high, taps_low = split_words(tap_rows)
    width = value_t.shape[2]
    taps_slab = jnp.pad(jnp.concatenate([taps_high, taps_low], axis=0).T, ((0, 0), (0, width - 2 * tap_count)))
    taps_slab = jnp.broadcast_to(taps_slab[None], value_t.shape)
    outs = jnp.stack([grad_gate, grad_key, grad_value, grad_filter.astype(BF16), taps_slab])
    outs = lax.all_to_all(outs, SEQ, split_axis=1, concat_axis=1, tiled=True)
    taps_got = outs[4, :, :, : 2 * tap_count]
    grad_taps = join_words(taps_got[..., :tap_count], taps_got[..., tap_count:])
    grad_taps = jnp.transpose(grad_taps, (2, 0, 1)).reshape(tap_count, -1)
    outs = from_tokens_in_lanes(outs[:4])
    grad_filter = outs[3].astype(F32)

    blocks = value_t.shape[0]
    inputs_3 = inputs_all.reshape(blocks, width, inputs_all.shape[1])
    grad_proj = jnp.einsum("pmi,cpom->ico", inputs_3, value_cols, preferred_element_type=F32)
    grad_proj = grad_proj.reshape(grad_proj.shape[0], -1)
    return (outs[0], outs[1], outs[2], grad_taps, grad_filter, grad_proj)


def solution(mesh):
    seq_size, chan_size = mesh.shape[SEQ_NAME], mesh.shape[CHAN_NAME]
    assert seq_size == chan_size and seq_size % 4 == 0 and chan_size % 2 == 0
    grid = mesh.devices.reshape(4, seq_size // 4, chan_size // 2, 2)
    fine = jax.sharding.Mesh(grid, SEQ + CHAN)
    rows = P(SEQ, CHAN)
    in_specs = (rows, rows, rows, rows, P(None, CHAN), rows, rows)
    out_specs = (rows, rows, rows, P(None, CHAN), rows, P(CHAN, SEQ))
    return jax.shard_map(on_device, mesh=fine, in_specs=in_specs, out_specs=out_specs, check_vma=False)
```

```python
import numpy as np

import jax
import jax.numpy as jnp
from jax import lax
from jax.sharding import PartitionSpec as P


F32 = jnp.float32
BF16 = jnp.bfloat16
PRECISE = lax.Precision.HIGH
SEQ = ("y", "x")
SEQ_NAME, CHAN_NAME = "seq", "chan"
CHAN = ("z", "core")


def angles(rows, cols, period):
    product = np.outer(np.arange(rows), np.arange(cols)) % period
    return product.astype(np.float64) * (2.0 * np.pi / period)


def dft_tables(blocks, width):
    freq_blocks = 2 * blocks
    total = freq_blocks * width
    outer = angles(freq_blocks, blocks, freq_blocks)
    stage_a = np.concatenate([np.cos(outer), -np.sin(outer)], axis=0)
    twist = angles(freq_blocks, width, total)
    twist_cos = np.cos(twist)[:, None, None, :]
    twist_sin = np.sin(twist)[:, None, None, :]
    back_a = np.concatenate([np.cos(outer).T, -np.sin(outer).T], axis=1) / total
    as_f32 = lambda a: jnp.asarray(a.astype(np.float32))
    rows = lax.broadcasted_iota(jnp.int32, (width, width), 0)
    cols = lax.broadcasted_iota(jnp.int32, (width, width), 1)
    product = lax.optimization_barrier(rows * cols % width)
    inner = product.astype(F32) * (2.0 * np.pi / width)
    inner_cos, inner_sin = jnp.cos(inner), jnp.sin(inner)
    stage_b = jnp.concatenate(
        [jnp.concatenate([inner_cos, -inner_sin], axis=1), jnp.concatenate([inner_sin, inner_cos], axis=1)],
        axis=0,
    )
    back_b = jnp.concatenate(
        [jnp.concatenate([inner_cos, inner_sin], axis=1), jnp.concatenate([-inner_sin, inner_cos], axis=1)],
        axis=0,
    )
    stage_a, twist_cos, twist_sin, back_a = (as_f32(a) for a in (stage_a, twist_cos, twist_sin, back_a))
    return stage_a, twist_cos, twist_sin, stage_b, back_b, back_a


def spectra(stacked, tables):
    stage_a, twist_cos, twist_sin, stage_b, _, _ = tables
    freq_blocks = 2 * stacked.shape[0]
    width = stacked.shape[-1]
    outer = jnp.einsum("kp,pscm->kscm", stage_a, stacked, precision=PRECISE)
    outer_re, outer_im = outer[:freq_blocks], outer[freq_blocks:]
    turned_re = outer_re * twist_cos + outer_im * twist_sin
    turned_im = outer_im * twist_cos - outer_re * twist_sin
    spec = jnp.einsum("kscm,mn->kscn", turned_re, stage_b[:width], precision=PRECISE) + jnp.einsum(
        "kscm,mn->kscn", turned_im, stage_b[width:], precision=PRECISE
    )
    return spec[..., :width], spec[..., width:]


def signals_back(prod_re, prod_im, tables):
    _, twist_cos, twist_sin, _, back_b, back_a = tables
    width = prod_re.shape[-1]
    inner = jnp.einsum("kscn,nm->kscm", prod_re, back_b[:width], precision=PRECISE) + jnp.einsum(
        "kscn,nm->kscm", prod_im, back_b[width:], precision=PRECISE
    )
    inner_re, inner_im = inner[..., :width], inner[..., width:]
    back_re = inner_re * twist_cos - inner_im * twist_sin
    back_im = inner_re * twist_sin + inner_im * twist_cos
    both = jnp.concatenate([back_re, back_im], axis=0)
    return jnp.einsum("pk,kscm->pscm", back_a, both, precision=PRECISE)


def shift_back(x, by, lane):
    earlier = jnp.concatenate([jnp.zeros_like(x[:1]), x[:-1]], axis=0)
    return jnp.where(lane < by, jnp.roll(earlier, by, axis=-1), jnp.roll(x, by, axis=-1))


def shift_ahead(x, by, lane):
    later = jnp.concatenate([x[1:], jnp.zeros_like(x[:1])], axis=0)
    width = x.shape[-1]
    return jnp.where(lane >= width - by, jnp.roll(later, -by, axis=-1), jnp.roll(x, -by, axis=-1))


def to_tokens_in_lanes(block, parts):
    rows, cols = block.shape[-2:]
    swapped = jnp.swapaxes(block, -1, -2)
    return swapped.reshape(block.shape[:-2] + (parts, cols // parts, rows))


def from_tokens_in_lanes(block):
    lead = block.shape[:-3]
    parts, sub, rows = block.shape[-3:]
    return jnp.swapaxes(block.reshape(lead + (parts * sub, rows)), -1, -2)


def split_words(x):
    rounded = lax.reduce_precision(x, exponent_bits=8, mantissa_bits=7)
    return rounded.astype(BF16), (x - rounded).astype(BF16)


def join_words(high, low):
    return high.astype(F32) + low.astype(F32)


def on_device(layer_input, value_pre, gate_act, key_act, short_taps, long_filter, grad_out):
    n_seq = lax.axis_size(SEQ)
    n_chan = lax.axis_size(CHAN)
    me = lax.axis_index(SEQ)
    tap_count = short_taps.shape[0]
    sub = value_pre.shape[1] // n_seq

    inputs_all = lax.all_gather(layer_input, "x", axis=0, tiled=True)
    inputs_all = lax.all_gather(inputs_all, "y", axis=0, tiled=True)

    filt_high, filt_low = split_words(long_filter)
    sent = to_tokens_in_lanes(jnp.stack([value_pre, gate_act, key_act, grad_out, filt_high, filt_low]), n_seq)
    got = lax.all_to_all(sent, SEQ, split_axis=1, concat_axis=1, tiled=True)
    value_t = got[0].astype(F32)
    gate_t = got[1].astype(F32)
    key_t = got[2].astype(F32)
    gout_t = got[3].astype(F32)
    filt = join_words(got[4], got[5])
    taps = lax.dynamic_slice_in_dim(short_taps, me * sub, sub, axis=1)[:, :, None]
    lane = lax.broadcasted_iota(jnp.int32, value_t.shape, 2)

    value_shifted = [value_t] + [shift_back(value_t, j, lane) for j in range(1, tap_count)]
    conv_val = taps[0] * value_shifted[0]
    for tap_index in range(1, tap_count):
        conv_val = conv_val + taps[tap_index] * value_shifted[tap_index]
    signal = key_t * conv_val
    grad_mix = gout_t * gate_t
    tables = dft_tables(value_t.shape[0], value_t.shape[2])
    fg_re, fg_im = spectra(jnp.stack([filt, grad_mix], axis=1), tables)
    filt_re, grad_re = fg_re[:, 0:1], fg_re[:, 1:2]
    filt_im, grad_im = fg_im[:, 0:1], fg_im[:, 1:2]
    grad_signal = signals_back(
        filt_re * grad_re + filt_im * grad_im, filt_re * grad_im - filt_im * grad_re, tables
    )[:, 0]
    grad_key = (grad_signal * conv_val).astype(BF16)
    grad_conv = grad_signal * key_t
    value_sum = taps[0] * grad_conv
    for tap_index in range(1, tap_count):
        value_sum = value_sum + taps[tap_index] * shift_ahead(grad_conv, tap_index, lane)
    grad_value = value_sum.astype(BF16)

    grad_value, signal, filt_re, filt_im, grad_re, grad_im = lax.optimization_barrier(
        (grad_value, signal, filt_re, filt_im, grad_re, grad_im)
    )
    swap = [(a * n_chan + b, b * n_chan + a) for a in range(n_seq) for b in range(n_chan)]
    value_swapped = lax.ppermute(grad_value, SEQ + CHAN, swap)
    value_cols = lax.all_gather(value_swapped, CHAN, axis=0, tiled=False)

    sig_re, sig_im = spectra(signal[:, None], tables)
    prod_re = jnp.concatenate(
        [filt_re * sig_re - filt_im * sig_im, sig_re * grad_re + sig_im * grad_im], axis=1
    )
    prod_im = jnp.concatenate(
        [filt_re * sig_im + filt_im * sig_re, sig_re * grad_im - sig_im * grad_re], axis=1
    )
    mixed = signals_back(prod_re, prod_im, tables)
    mix_out, grad_filter = mixed[:, 0], mixed[:, 1]
    grad_gate = (gout_t * mix_out).astype(BF16)

    tap_rows = jnp.stack([jnp.sum(grad_conv * value_shifted[j], axis=(0, 2)) for j in range(tap_count)])
    taps_high, taps_low = split_words(tap_rows)
    width = value_t.shape[2]
    taps_slab = jnp.pad(jnp.concatenate([taps_high, taps_low], axis=0).T, ((0, 0), (0, width - 2 * tap_count)))
    taps_slab = jnp.broadcast_to(taps_slab[None], value_t.shape)
    gf_high, gf_low = split_words(grad_filter)
    outs = jnp.stack([grad_gate, grad_key, grad_value, gf_high, gf_low, taps_slab])
    outs = lax.all_to_all(outs, SEQ, split_axis=1, concat_axis=1, tiled=True)
    taps_got = outs[5, :, :, : 2 * tap_count]
    grad_taps = join_words(taps_got[..., :tap_count], taps_got[..., tap_count:])
    grad_taps = jnp.transpose(grad_taps, (2, 0, 1)).reshape(tap_count, -1)
    outs = from_tokens_in_lanes(outs[:5])
    grad_filter = join_words(outs[3], outs[4])

    blocks = value_t.shape[0]
    inputs_3 = inputs_all.reshape(blocks, width, inputs_all.shape[1])
    grad_proj = jnp.einsum("pmi,cpom->ico", inputs_3, value_cols, preferred_element_type=F32)
    grad_proj = grad_proj.reshape(grad_proj.shape[0], -1)
    return (outs[0], outs[1], outs[2], grad_taps, grad_filter, grad_proj)


def solution(mesh):
    seq_size, chan_size = mesh.shape[SEQ_NAME], mesh.shape[CHAN_NAME]
    assert seq_size == chan_size and seq_size % 4 == 0 and chan_size % 2 == 0
    grid = mesh.devices.reshape(4, seq_size // 4, chan_size // 2, 2)
    fine = jax.sharding.Mesh(grid, SEQ + CHAN)
    rows = P(SEQ, CHAN)
    in_specs = (rows, rows, rows, rows, P(None, CHAN), rows, rows)
    out_specs = (rows, rows, rows, P(None, CHAN), rows, P(CHAN, SEQ))
    return jax.shard_map(on_device, mesh=fine, in_specs=in_specs, out_specs=out_specs, check_vma=False)
```
